32 devices in a mesh: node: 4 (over y, core), local: 8 (over z, x).
Axes of the slice: x: 2, y: 2, z: 4, core: 2. Of those that a mesh axis runs over, the one named last changes fastest.
Arguments:
- tokens: bfloat16 [4096, 4096], P(('node', 'local')), may hold values from -6 to 6
- grad_out: bfloat16 [4096, 4096], P(('node', 'local')), may hold values from -6 to 6
- expert_ids: int32 [4096, 4], P(('node', 'local')), may hold values from 0 to 31, all different within a row; in each aligned block of 128 rows (0 to 127, 128 to 255, ...) at most 20 rows name the same one
- combine_w: float32 [4096, 4], P(('node', 'local')), may hold values from 0.1 to 0.6
- w_gate: bfloat16 [32, 4096, 768], P(('node', 'local')), may hold values from -0.09375 to 0.09375
- w_up: bfloat16 [32, 4096, 768], P(('node', 'local')), may hold values from -0.09375 to 0.09375
- w_down: bfloat16 [32, 768, 4096], P(('node', 'local')), may hold values from -0.21875 to 0.21875
Outputs:
- mixed: bfloat16 [4096, 4096], P(('node', 'local'))
- grad_in: bfloat16 [4096, 4096], P(('node', 'local'))
The draws below stay inside these ranges and needn't reach their ends.
Inputs may be any that keep to these rules, and one draw needn't show every extreme that they name: `expert_ids`: each row names 4 different experts. Among the 128 rows of one device no expert is named more than 20 times, and in every draw some device names some expert exactly 20 times.
All inputs are finite; a program needn't handle non-finite values.
Results may differ from the reference program's by a relative error of at most 0.0058.
Values may be sent and summed in bfloat16 or wider, within the bound.
No kernel may reach another device: no remote copies, remote signals or barrier semaphores. Data moves between devices by JAX's collectives and lax.ppermute only.
A program may use at most 128 MiB of HBM per device.

```python
import math
import jax
import jax.numpy as jnp
import numpy as np
from jax import lax

D = 4096
FF = 768
TOPK = 4
TOK_DEV = 128
EXPERTS = 32
TOKENS = 4096
CAP = 20
N_NODE = 4
N_LOCAL = 8


def block_levels(rng, dims, cuts, low, top_value):
    gain, own = 1.0, jax.random.fold_in(rng, 6)
    for position, shards_of in cuts:
        heights = jnp.exp(jax.random.uniform(jax.random.fold_in(own, position), (shards_of,), jnp.float32, low / len(cuts), top_value / len(cuts)))
        gain = gain * jnp.repeat(heights, dims[position] // shards_of).reshape([-1 if axis == position else 1 for axis in range(len(dims))])
    return gain


def deal_out(rng, own, number, rows, amount, top, most, slope):
    sequence = jax.random.permutation(rng, amount)
    packed, usual = portions_of(amount, rows * top, most, slope, True), portions_of(amount, rows * top, most, slope, False)
    places = jnp.arange(amount)

    def named(lengths, offset_by):
        used = int((lengths > 0).sum())
        fixed = max(1, used // 4)
        passed = fixed + (places - fixed + offset_by * (used - fixed)) % max(1, amount - fixed)
        return jnp.zeros((amount,), jnp.int32).at[sequence[jnp.where(places < fixed, places, passed)]].set(jnp.asarray(lengths, jnp.int32))

    lengths = jnp.where(number % 4 == 0, named(packed, number // 4), named(usual, number - number // 4 - 1))
    mixed = jax.random.permutation(jax.random.fold_in(own, 3), amount)
    donor, taker = mixed[0:amount // 2 * 2:2], mixed[1:amount // 2 * 2:2]
    room = jnp.minimum(lengths[donor] - 1, most - lengths[taker]) // 2
    room = jnp.where((donor == sequence[0]) | (taker == sequence[0]) | (lengths[taker] == 0), 0, jnp.maximum(room, 0))
    passed = jax.random.randint(jax.random.fold_in(own, 4), (amount // 2,), 0, 1 << 20) % (room + 1)
    lengths = lengths.at[donor].add(-passed).at[taker].add(passed)
    members = jnp.searchsorted(jnp.cumsum(lengths), jnp.arange(rows * top), side="right").astype(jnp.int32)
    grid = members.reshape(top, rows).T
    grid = grid[jax.random.permutation(jax.random.fold_in(own, 1), rows)]
    offset_by = jax.random.randint(jax.random.fold_in(own, 2), (rows, 1), 0, top)
    return jnp.take_along_axis(grid, (jnp.arange(top)[None, :] + offset_by) % top, axis=1)


def portions_of(count, total, most, skew, full):
    loads = [(1 << 20) // math.isqrt(grade ** skew) + 1 for grade in range(1, count + 1)]
    largest = most if full else min(most, max(-(-total // count), total * loads[0] // sum(loads)))
    least = 1 if total - largest >= count - 1 else 0
    holding, rest = [largest] + [least] * (count - 1), total - largest - least * (count - 1)
    while rest > 0:
        movable = [i for i in range(1, count) if holding[i] < largest] or [i for i in range(1, count) if holding[i] < most]
        whole, remaining = sum([loads[i] for i in movable]), rest
        for i in movable:
            addition = min(most - holding[i], max(1, remaining * loads[i] // whole), rest)
            holding[i] = holding[i] + addition
            rest = rest - addition
    return np.array(holding)


def bell_draw(stream_key, extent, spread, most, shards=(), kind=jnp.bfloat16):
    drawn = spread * jax.random.normal(stream_key, extent, jnp.float32)
    if shards:
        drawn = drawn * block_levels(stream_key, extent, shards, -0.22, 0.18)
    return jnp.clip(drawn, -most, most).astype(kind)


def setup_inputs(seed: int = 0) -> dict:
    splits = jax.random.split(jax.random.key(seed), 8)
    tokens = bell_draw(splits[0], (TOKENS, D), 1.0, 6.0, ((0, 32),))
    grad_out = bell_draw(splits[1], (TOKENS, D), 1.0, 6.0, ((0, 32),))
    expert_ids_keys = jax.random.split(jax.random.fold_in(splits[2], 1), TOKENS // TOK_DEV)
    expert_ids_turns = jax.random.permutation(jax.random.fold_in(splits[2], 3), TOKENS // TOK_DEV)
    expert_ids = jax.vmap(lambda own, number: deal_out(jax.random.fold_in(splits[2], 2), own, number, TOK_DEV, EXPERTS, TOPK, CAP, 2))(expert_ids_keys, expert_ids_turns).reshape((TOKENS, TOPK))
    combine_w = jnp.clip(0.1 + 0.5 * jax.random.uniform(splits[3], (TOKENS, TOPK), jnp.float32) ** block_levels(splits[3], (TOKENS, TOPK), ((0, 32),), -0.2, 0.2), 0.1, 0.6)
    w_gate = bell_draw(splits[4], (EXPERTS, D, FF), D ** -0.5, 0.09375, ((0, 32),))
    w_up = bell_draw(splits[5], (EXPERTS, D, FF), D ** -0.5, 0.09375, ((0, 32),))
    w_down = bell_draw(splits[6], (EXPERTS, FF, D), FF ** -0.5, 0.21875, ((0, 32),))
    return dict(tokens=tokens, grad_out=grad_out, expert_ids=expert_ids, combine_w=combine_w, w_gate=w_gate, w_up=w_up, w_down=w_down)


def expert_rows(rows, gate_w, up_w, down_w, width):
    inputs = rows[:, :width]
    upstream = rows[:, width:]
    gate = jnp.dot(inputs, gate_w, preferred_element_type=jnp.float32)
    lifted = jnp.dot(inputs, up_w, preferred_element_type=jnp.float32)
    sigma = jax.nn.sigmoid(gate)
    active = (gate * sigma * lifted).astype(jnp.bfloat16)
    result = jnp.dot(active, down_w, preferred_element_type=jnp.float32).astype(jnp.bfloat16)
    contract = (((1,), (1,)), ((), ()))
    back = lax.dot_general(upstream, down_w, contract, preferred_element_type=jnp.float32)
    d_gate = (back * lifted * sigma * (1.0 + gate * (1.0 - sigma))).astype(jnp.bfloat16)
    d_lift = (back * gate * sigma).astype(jnp.bfloat16)
    grads = lax.dot_general(d_gate, gate_w, contract, preferred_element_type=jnp.float32)
    grads = grads + lax.dot_general(d_lift, up_w, contract, preferred_element_type=jnp.float32)
    return jnp.concatenate([result, grads.astype(jnp.bfloat16)], axis=1)


def reference(tokens, grad_out, expert_ids, combine_w, w_gate, w_up, w_down):
    devices = N_NODE * N_LOCAL
    per_device = TOK_DEV * TOPK
    ids = expert_ids.reshape(devices, per_device).astype(jnp.int32)
    onehot = (ids[:, :, None] == jnp.arange(EXPERTS, dtype=jnp.int32)[None, None, :]).astype(jnp.int32)
    ranks = jnp.sum((jnp.cumsum(onehot, axis=1) - 1) * onehot, axis=2)
    column = jnp.arange(devices, dtype=jnp.int32)[:, None] * CAP + ranks
    assign = jnp.arange(TOKENS * TOPK, dtype=jnp.int32).reshape(devices, per_device)
    table = jnp.full((EXPERTS, devices * CAP), TOKENS * TOPK, jnp.int32).at[ids, column].set(assign)
    paired = jnp.concatenate([tokens, grad_out], axis=1)
    paired = jnp.concatenate([paired, jnp.zeros((1, 2 * D), jnp.bfloat16)], axis=0)
    weights = jnp.concatenate([combine_w.reshape(-1), jnp.zeros((1,), jnp.float32)])

    def visit(total, items):
        gate_w, up_w, down_w, entries = items
        owners = (entries // TOPK).astype(jnp.int32)
        rows = expert_rows(paired[owners], gate_w, up_w, down_w, D)
        total = total.at[owners].add(rows.astype(jnp.float32) * weights[entries][:, None])
        return total, None

    start = jnp.zeros((TOKENS + 1, 2 * D), jnp.float32)
    total, _ = lax.scan(visit, start, (w_gate, w_up, w_down, table))
    return total[:TOKENS, :D].astype(jnp.bfloat16), total[:TOKENS, D:].astype(jnp.bfloat16)
```

```python
import jax
import jax.numpy as jnp
from jax import lax
from jax.sharding import PartitionSpec as P


def expert_rows(rows, gate_w, up_w, down_w, width):
    inputs = rows[:, :width]
    upstream = rows[:, width:]
    gate = jnp.dot(inputs, gate_w, preferred_element_type=jnp.float32)
    lifted = jnp.dot(inputs, up_w, preferred_element_type=jnp.float32)
    sigma = jax.nn.sigmoid(gate)
    active = (gate * sigma * lifted).astype(jnp.bfloat16)
    result = jnp.dot(active, down_w, preferred_element_type=jnp.float32).astype(jnp.bfloat16)
    contract = (((1,), (1,)), ((), ()))
    back = lax.dot_general(upstream, down_w, contract, preferred_element_type=jnp.float32)
    d_gate = (back * lifted * sigma * (1.0 + gate * (1.0 - sigma))).astype(jnp.bfloat16)
    d_lift = (back * gate * sigma).astype(jnp.bfloat16)
    grads = lax.dot_general(d_gate, gate_w, contract, preferred_element_type=jnp.float32)
    grads = grads + lax.dot_general(d_lift, up_w, contract, preferred_element_type=jnp.float32)
    return jnp.concatenate([result, grads.astype(jnp.bfloat16)], axis=1)


def row_slots(expert_ids, experts, capacity):
    flat_ids = expert_ids.reshape(-1)
    onehot = (flat_ids[:, None] == jnp.arange(experts, dtype=jnp.int32)[None, :]).astype(jnp.int32)
    ranks = jnp.sum((jnp.cumsum(onehot, axis=0) - 1) * onehot, axis=1)
    return flat_ids * capacity + ranks


def outward(buffer):
    return lax.all_to_all(buffer, ("node", "local"), split_axis=0, concat_axis=0, tiled=True)


def homeward(buffer):
    return lax.all_to_all(buffer, ("node", "local"), split_axis=0, concat_axis=0, tiled=True)


def split_three(weights):
    high = weights.astype(jnp.bfloat16)
    rest = weights - high.astype(jnp.float32)
    middle = rest.astype(jnp.bfloat16)
    low = (rest - middle.astype(jnp.float32)).astype(jnp.bfloat16)
    return high, middle, low


def per_device(tokens, grad_out, expert_ids, combine_w, w_gate, w_up, w_down):
    token_count, width = tokens.shape
    top_count = expert_ids.shape[1]
    experts = lax.axis_size("node") * lax.axis_size("local")
    capacity = max(2, (5 * token_count * top_count + 4 * experts - 1) // (4 * experts))
    slots_per = (capacity + 7) // 8 * 8
    total_slots = experts * slots_per
    slots = row_slots(expert_ids, experts, slots_per).reshape(token_count, top_count)
    hits = slots[None, :, :] == jnp.arange(total_slots, dtype=jnp.int32)[:, None, None]
    dispatch = jnp.any(hits, axis=2).astype(jnp.bfloat16)
    paired = jnp.concatenate([tokens, grad_out], axis=1)
    buffer = jnp.dot(dispatch, paired, preferred_element_type=jnp.float32).astype(jnp.bfloat16)
    received = outward(buffer.reshape(experts, slots_per, 2 * width))
    received = received.reshape(total_slots, 2 * width)
    produced = expert_rows(received, w_gate[0], w_up[0], w_down[0], width)
    returned = homeward(produced.reshape(experts, slots_per, 2 * width))
    returned = returned.reshape(total_slots, 2 * width)
    spread = jnp.where(hits, combine_w[None, :, :], 0.0).sum(axis=2).T
    summed = None
    for part in split_three(spread):
        term = jnp.dot(part, returned, preferred_element_type=jnp.float32)
        summed = term if summed is None else summed + term
    return (summed[:, :width].astype(jnp.bfloat16), summed[:, width:].astype(jnp.bfloat16))


def solution(mesh):
    return jax.shard_map(
        per_device,
        mesh=mesh,
        in_specs=(
            P(("node", "local"), None),
            P(("node", "local"), None),
            P(("node", "local"), None),
            P(("node", "local"), None),
            P(("node", "local"), None, None),
            P(("node", "local"), None, None),
            P(("node", "local"), None, None),
        ),
        out_specs=(P(("node", "local"), None), P(("node", "local"), None)),
        check_vma=False,
    )
```

```python
import jax
import jax.numpy as jnp
from jax import lax
from jax.sharding import PartitionSpec as P


def expert_rows(inputs, upstream, gate_w, up_w, down_w):
    gate = jnp.dot(inputs, gate_w, preferred_element_type=jnp.float32)
    lifted = jnp.dot(inputs, up_w, preferred_element_type=jnp.float32)
    sigma = jax.nn.sigmoid(gate)
    active = (gate * sigma * lifted).astype(jnp.bfloat16)
    result = jnp.dot(active, down_w, preferred_element_type=jnp.float32).astype(jnp.bfloat16)
    contract = (((1,), (1,)), ((), ()))
    back = lax.dot_general(upstream, down_w, contract, preferred_element_type=jnp.float32)
    d_gate = (back * lifted * sigma * (1.0 + gate * (1.0 - sigma))).astype(jnp.bfloat16)
    d_lift = (back * gate * sigma).astype(jnp.bfloat16)
    grads = lax.dot_general(d_gate, gate_w, contract, preferred_element_type=jnp.float32)
    grads = grads + lax.dot_general(d_lift, up_w, contract, preferred_element_type=jnp.float32)
    return jnp.stack([result, grads.astype(jnp.bfloat16)], axis=1)


def row_slots(expert_ids, experts, capacity):
    flat_ids = expert_ids.reshape(-1)
    onehot = (flat_ids[:, None] == jnp.arange(experts, dtype=jnp.int32)[None, :]).astype(jnp.int32)
    ranks = jnp.sum((jnp.cumsum(onehot, axis=0) - 1) * onehot, axis=1)
    return flat_ids * capacity + ranks


def outward(buffer):
    return lax.all_to_all(buffer, ("node", "local"), split_axis=0, concat_axis=0, tiled=True)


def homeward(buffer):
    return lax.all_to_all(buffer, ("node", "local"), split_axis=0, concat_axis=0, tiled=True)


def split_three(weights):
    high = lax.reduce_precision(weights, exponent_bits=8, mantissa_bits=7)
    rest = weights - high
    middle = lax.reduce_precision(rest, exponent_bits=8, mantissa_bits=7)
    low = rest - middle
    return [part.astype(jnp.bfloat16) for part in (high, middle, low)]


def per_device(tokens, grad_out, expert_ids, combine_w, w_gate, w_up, w_down):
    token_count, width = tokens.shape
    top_count = expert_ids.shape[1]
    experts = lax.axis_size("node") * lax.axis_size("local")
    capacity = max(2, (5 * token_count * top_count + 4 * experts - 1) // (4 * experts))
    slots_per = (capacity + 3) // 4 * 4
    total_slots = experts * slots_per
    slots = row_slots(expert_ids, experts, slots_per).reshape(token_count, top_count)
    hits = slots[None, :, :] == jnp.arange(total_slots, dtype=jnp.int32)[:, None, None]
    taken = jnp.any(hits, axis=2).astype(jnp.bfloat16)
    blank = jnp.zeros_like(taken)
    dispatch = jnp.stack([jnp.concatenate([taken, blank], axis=1), jnp.concatenate([blank, taken], axis=1)], axis=1)
    dispatch = dispatch.reshape(2 * total_slots, 2 * token_count)
    stacked = jnp.concatenate([tokens, grad_out], axis=0)
    buffer = jnp.dot(dispatch, stacked, preferred_element_type=jnp.float32).astype(jnp.bfloat16)
    received = outward(buffer.reshape(experts, 2 * slots_per, width))
    received = received.reshape(total_slots, 2, width)
    produced = expert_rows(received[:, 0, :], received[:, 1, :], w_gate[0], w_up[0], w_down[0])
    returned = homeward(produced.reshape(experts, 2 * slots_per, width))
    returned = returned.reshape(2 * total_slots, width)
    spread = jnp.where(hits, combine_w[None, :, :], 0.0).sum(axis=2).T
    zero = jnp.zeros_like(spread)
    weights = jnp.concatenate([jnp.stack([spread, zero], axis=2), jnp.stack([zero, spread], axis=2)], axis=0)
    weights = weights.reshape(2 * token_count, 2 * total_slots)
    summed = jnp.dot(jnp.concatenate(split_three(weights), axis=0), returned, preferred_element_type=jnp.float32)
    summed = summed.reshape(3, 2 * token_count, width).sum(axis=0)
    return (summed[:token_count].astype(jnp.bfloat16), summed[token_count:].astype(jnp.bfloat16))


def solution(mesh):
    return jax.shard_map(
        per_device,
        mesh=mesh,
        in_specs=(
            P(("node", "local"), None),
            P(("node", "local"), None),
            P(("node", "local"), None),
            P(("node", "local"), None),
            P(("node", "local"), None, None),
            P(("node", "local"), None, None),
            P(("node", "local"), None, None),
        ),
        out_specs=(P(("node", "local"), None), P(("node", "local"), None)),
        check_vma=False,
    )
```

```python
import jax
import jax.numpy as jnp
from jax import lax
from jax.sharding import PartitionSpec as P


def expert_rows(inputs, upstream, gate_w, up_w, down_w):
    gate = jnp.dot(inputs, gate_w, preferred_element_type=jnp.float32)
    lifted = jnp.dot(inputs, up_w, preferred_element_type=jnp.float32)
    sigma = jax.nn.sigmoid(gate)
    active = (gate * sigma * lifted).astype(jnp.bfloat16)
    result = jnp.dot(active, down_w, preferred_element_type=jnp.float32).astype(jnp.bfloat16)
    contract = (((1,), (1,)), ((), ()))
    back = lax.dot_general(upstream, down_w, contract, preferred_element_type=jnp.float32)
    d_gate = (back * lifted * sigma * (1.0 + gate * (1.0 - sigma))).astype(jnp.bfloat16)
    d_lift = (back * gate * sigma).astype(jnp.bfloat16)
    grads = lax.dot_general(d_gate, gate_w, contract, preferred_element_type=jnp.float32)
    grads = grads + lax.dot_general(d_lift, up_w, contract, preferred_element_type=jnp.float32)
    return result, grads.astype(jnp.bfloat16)


def row_slots(expert_ids, experts, capacity):
    flat_ids = expert_ids.reshape(-1)
    onehot = (flat_ids[:, None] == jnp.arange(experts, dtype=jnp.int32)[None, :]).astype(jnp.int32)
    ranks = jnp.sum((jnp.cumsum(onehot, axis=0) - 1) * onehot, axis=1)
    return flat_ids * capacity + ranks


def outward(buffer):
    return lax.all_to_all(buffer, ("node", "local"), split_axis=0, concat_axis=0, tiled=True)


def homeward(buffer):
    return lax.all_to_all(buffer, ("node", "local"), split_axis=0, concat_axis=0, tiled=True)


def split_three(weights):
    high = lax.reduce_precision(weights, exponent_bits=8, mantissa_bits=7)
    rest = weights - high
    middle = lax.reduce_precision(rest, exponent_bits=8, mantissa_bits=7)
    low = rest - middle
    return [part.astype(jnp.bfloat16) for part in (high, middle, low)]


def per_device(tokens, grad_out, expert_ids, combine_w, w_gate, w_up, w_down):
    token_count, width = tokens.shape
    top_count = expert_ids.shape[1]
    experts = lax.axis_size("node") * lax.axis_size("local")
    capacity = max(2, (5 * token_count * top_count + 4 * experts - 1) // (4 * experts))
    slots_per = (capacity + 3) // 4 * 4
    main = slots_per // 8 * 8
    tail = slots_per - main
    chunk = 2 * slots_per
    slots = row_slots(expert_ids, experts, slots_per).reshape(token_count, top_count)
    place = jnp.arange(chunk, dtype=jnp.int32)
    in_tail = place >= 2 * main
    rank = jnp.where(in_tail, main + (place - 2 * main) % jnp.maximum(tail, 1), place % jnp.maximum(main, 1))
    part = jnp.where(in_tail, (place - 2 * main) // jnp.maximum(tail, 1), place // jnp.maximum(main, 1))
    row_slot = (jnp.arange(experts, dtype=jnp.int32)[:, None] * slots_per + rank[None, :]).reshape(-1)
    row_part = jnp.tile(part, experts)
    hits = slots[None, :, :] == row_slot[:, None, None]
    taken = jnp.any(hits, axis=2).astype(jnp.bfloat16)
    blank = jnp.zeros_like(taken)
    first = (row_part == 0)[:, None]
    dispatch = jnp.concatenate([jnp.where(first, taken, blank), jnp.where(first, blank, taken)], axis=1)
    stacked = jnp.concatenate([tokens, grad_out], axis=0)
    buffer = jnp.dot(dispatch, stacked, preferred_element_type=jnp.float32).astype(jnp.bfloat16)
    received = outward(buffer.reshape(experts, chunk, width))
    inputs = received[:, :main].reshape(experts * main, width)
    upstream = received[:, main:2 * main].reshape(experts * main, width)
    if tail:
        ends = received[:, 2 * main:].reshape(experts, 2, tail, width)
        inputs = jnp.concatenate([inputs, ends[:, 0].reshape(experts * tail, width)], axis=0)
        upstream = jnp.concatenate([upstream, ends[:, 1].reshape(experts * tail, width)], axis=0)
    result, grads = expert_rows(inputs, upstream, w_gate[0], w_up[0], w_down[0])
    pieces = [result[:experts * main].reshape(experts, main, width), grads[:experts * main].reshape(experts, main, width)]
    if tail:
        pieces += [result[experts * main:].reshape(experts, tail, width), grads[experts * main:].reshape(experts, tail, width)]
    produced = jnp.concatenate(pieces, axis=1)
    returned = homeward(produced).reshape(experts * chunk, width)
    spread = jnp.where(hits, combine_w[None, :, :], 0.0).sum(axis=2).T
    zero = jnp.zeros_like(spread)
    first = (row_part == 0)[None, :]
    weights = jnp.concatenate([jnp.where(first, spread, zero), jnp.where(first, zero, spread)], axis=0)
    summed = jnp.dot(jnp.concatenate(split_three(weights), axis=0), returned, preferred_element_type=jnp.float32)
    summed = summed.reshape(3, 2 * token_count, width).sum(axis=0)
    return (summed[:token_count].astype(jnp.bfloat16), summed[token_count:].astype(jnp.bfloat16))


def solution(mesh):
    return jax.shard_map(
        per_device,
        mesh=mesh,
        in_specs=(
            P(("node", "local"), None),
            P(("node", "local"), None),
            P(("node", "local"), None),
            P(("node", "local"), None),
            P(("node", "local"), None, None),
            P(("node", "local"), None, None),
            P(("node", "local"), None, None),
        ),
        out_specs=(P(("node", "local"), None), P(("node", "local"), None)),
        check_vma=False,
    )
```

```python
import jax
import jax.numpy as jnp
from jax import lax
from jax.sharding import PartitionSpec as P


def expert_rows(inputs, upstream, gate_w, up_w, down_w):
    gate = jnp.dot(inputs, gate_w, preferred_element_type=jnp.float32)
    lifted = jnp.dot(inputs, up_w, preferred_element_type=jnp.float32)
    sigma = jax.nn.sigmoid(gate)
    active = (gate * sigma * lifted).astype(jnp.bfloat16)
    result = jnp.dot(active, down_w, preferred_element_type=jnp.float32).astype(jnp.bfloat16)
    contract = (((1,), (1,)), ((), ()))
    back = lax.dot_general(upstream, down_w, contract, preferred_element_type=jnp.float32)
    d_gate = (back * lifted * sigma * (1.0 + gate * (1.0 - sigma))).astype(jnp.bfloat16)
    d_lift = (back * gate * sigma).astype(jnp.bfloat16)
    grads = lax.dot_general(d_gate, gate_w, contract, preferred_element_type=jnp.float32)
    grads = grads + lax.dot_general(d_lift, up_w, contract, preferred_element_type=jnp.float32)
    return result, grads.astype(jnp.bfloat16)


def row_slots(expert_ids, experts, capacity):
    flat_ids = expert_ids.reshape(-1)
    onehot = (flat_ids[:, None] == jnp.arange(experts, dtype=jnp.int32)[None, :]).astype(jnp.int32)
    ranks = jnp.sum((jnp.cumsum(onehot, axis=0) - 1) * onehot, axis=1)
    return flat_ids * capacity + ranks


def inward(buffer):
    return lax.all_to_all(buffer, ("node", "sub"), split_axis=0, concat_axis=0, tiled=True)


def split_three(weights):
    high = lax.reduce_precision(weights, exponent_bits=8, mantissa_bits=7)
    rest = weights - high
    middle = lax.reduce_precision(rest, exponent_bits=8, mantissa_bits=7)
    low = rest - middle
    return [part.astype(jnp.bfloat16) for part in (high, middle, low)]


def per_device(tokens, grad_out, expert_ids, combine_w, w_gate, w_up, w_down):
    token_count, width = tokens.shape
    top_count = expert_ids.shape[1]
    halves = lax.axis_size("half")
    subs = lax.axis_size("sub")
    group_size = lax.axis_size("node") * subs
    experts = group_size * halves
    capacity = max(2, (5 * token_count * top_count + 4 * experts - 1) // (4 * experts))
    slots_per = (2 * capacity + 7) // 8 * 8
    total_slots = group_size * slots_per
    swap = [(i, (i + 1) % halves) for i in range(halves)]
    stacked = jnp.concatenate([tokens, grad_out], axis=0)
    far_stacked = lax.ppermute(stacked, "half", swap)
    ids = jnp.concatenate([expert_ids, lax.ppermute(expert_ids, "half", swap)], axis=0)
    wts = jnp.concatenate([combine_w, lax.ppermute(combine_w, "half", swap)], axis=0)
    near = (ids % (halves * subs)) // subs == lax.axis_index("half")
    group = (ids // (halves * subs)) * subs + ids % subs
    flat = jnp.where(near, group, group_size).reshape(-1)
    onehot = (flat[:, None] == jnp.arange(group_size, dtype=jnp.int32)[None, :]).astype(jnp.int32)
    ranks = jnp.sum((jnp.cumsum(onehot, axis=0) - 1) * onehot, axis=1)
    slots = jnp.where(flat < group_size, flat * slots_per + ranks, -1).reshape(2 * token_count, top_count)
    hits = slots[None, :, :] == jnp.arange(total_slots, dtype=jnp.int32)[:, None, None]
    taken = jnp.any(hits, axis=2).astype(jnp.bfloat16).reshape(group_size, 1, slots_per, 2 * token_count)
    blank = jnp.zeros_like(taken)
    dispatch = jnp.concatenate([jnp.concatenate([taken, blank], axis=3), jnp.concatenate([blank, taken], axis=3)], axis=1)
    dispatch = dispatch.reshape(2 * total_slots, 4 * token_count)
    source = jnp.concatenate([tokens, far_stacked[:token_count], grad_out, far_stacked[token_count:]], axis=0)
    buffer = jnp.dot(dispatch, source, preferred_element_type=jnp.float32).astype(jnp.bfloat16)
    received = inward(buffer.reshape(group_size, 2 * slots_per, width))
    inputs = received[:, :slots_per].reshape(total_slots, width)
    upstream = received[:, slots_per:].reshape(total_slots, width)
    result, grads = expert_rows(inputs, upstream, w_gate[0], w_up[0], w_down[0])
    produced = jnp.concatenate([result.reshape(group_size, slots_per, width), grads.reshape(group_size, slots_per, width)], axis=1)
    returned = inward(produced)
    spread = jnp.where(hits, wts[None, :, :], 0.0).sum(axis=2).T
    parts = jnp.concatenate(split_three(spread), axis=0)
    mixed = jnp.dot(parts, returned[:, :slots_per].reshape(total_slots, width), preferred_element_type=jnp.float32)
    grad_in = jnp.dot(parts, returned[:, slots_per:].reshape(total_slots, width), preferred_element_type=jnp.float32)
    mixed = mixed.reshape(3, 2 * token_count, width).sum(axis=0)
    grad_in = grad_in.reshape(3, 2 * token_count, width).sum(axis=0)
    far_part = jnp.concatenate([mixed[token_count:], grad_in[token_count:]], axis=0).astype(jnp.bfloat16)
    near_part = lax.ppermute(far_part, "half", swap).astype(jnp.float32)
    mixed = mixed[:token_count] + near_part[:token_count]
    grad_in = grad_in[:token_count] + near_part[token_count:]
    return (mixed.astype(jnp.bfloat16), grad_in.astype(jnp.bfloat16))


def solution(mesh):
    nodes = mesh.shape["node"]
    locals_ = mesh.shape["local"]
    grid = jax.sharding.Mesh(mesh.devices.reshape(nodes, 2, locals_ // 2), ("node", "half", "sub"))
    rows = P(("node", "half", "sub"), None)
    stack = P(("node", "half", "sub"), None, None)
    return jax.shard_map(
        per_device,
        mesh=grid,
        in_specs=(rows, rows, rows, rows, stack, stack, stack),
        out_specs=(rows, rows),
        check_vma=False,
    )
```

```python
import jax
import jax.numpy as jnp
from jax import lax
from jax.sharding import PartitionSpec as P


def expert_rows(inputs, upstream, gate_w, up_w, down_w):
    gate = jnp.dot(inputs, gate_w, preferred_element_type=jnp.float32)
    lifted = jnp.dot(inputs, up_w, preferred_element_type=jnp.float32)
    sigma = jax.nn.sigmoid(gate)
    active = (gate * sigma * lifted).astype(jnp.bfloat16)
    result = jnp.dot(active, down_w, preferred_element_type=jnp.float32).astype(jnp.bfloat16)
    contract = (((1,), (1,)), ((), ()))
    back = lax.dot_general(upstream, down_w, contract, preferred_element_type=jnp.float32)
    d_gate = (back * lifted * sigma * (1.0 + gate * (1.0 - sigma))).astype(jnp.bfloat16)
    d_lift = (back * gate * sigma).astype(jnp.bfloat16)
    grads = lax.dot_general(d_gate, gate_w, contract, preferred_element_type=jnp.float32)
    grads = grads + lax.dot_general(d_lift, up_w, contract, preferred_element_type=jnp.float32)
    return result, grads.astype(jnp.bfloat16)


def row_slots(expert_ids, experts, capacity):
    flat_ids = expert_ids.reshape(-1)
    onehot = (flat_ids[:, None] == jnp.arange(experts, dtype=jnp.int32)[None, :]).astype(jnp.int32)
    ranks = jnp.sum((jnp.cumsum(onehot, axis=0) - 1) * onehot, axis=1)
    return flat_ids * capacity + ranks


def inward(buffer):
    return lax.all_to_all(buffer, ("node", "sub"), split_axis=0, concat_axis=0, tiled=True)


def split_three(weights):
    high = lax.reduce_precision(weights, exponent_bits=8, mantissa_bits=7)
    rest = weights - high
    middle = lax.reduce_precision(rest, exponent_bits=8, mantissa_bits=7)
    low = rest - middle
    return [part.astype(jnp.bfloat16) for part in (high, middle, low)]


def chunk_rows(group_size, slots_per):
    main = slots_per // 8 * 8
    tail = slots_per - main
    place = jnp.arange(2 * slots_per, dtype=jnp.int32)
    in_tail = place >= 2 * main
    rank = jnp.where(in_tail, main + (place - 2 * main) % max(tail, 1), place % max(main, 1))
    part = jnp.where(in_tail, (place - 2 * main) // max(tail, 1), place // max(main, 1))
    row_slot = (jnp.arange(group_size, dtype=jnp.int32)[:, None] * slots_per + rank[None, :]).reshape(-1)
    return row_slot, jnp.tile(part, group_size) == 0


def route(ids, near, group, group_size, slots_per):
    flat = jnp.where(near, group, group_size).reshape(-1)
    onehot = (flat[:, None] == jnp.arange(group_size, dtype=jnp.int32)[None, :]).astype(jnp.int32)
    ranks = jnp.sum((jnp.cumsum(onehot, axis=0) - 1) * onehot, axis=1)
    return jnp.where(flat < group_size, flat * slots_per + ranks, -1).reshape(ids.shape)


def pack(slots, inputs, upstream, row_slot, first):
    hits = slots[None, :, :] == row_slot[:, None, None]
    taken = jnp.any(hits, axis=2).astype(jnp.bfloat16)
    blank = jnp.zeros_like(taken)
    dispatch = jnp.concatenate([jnp.where(first[:, None], taken, blank), jnp.where(first[:, None], blank, taken)], axis=1)
    source = jnp.concatenate([inputs, upstream], axis=0)
    return jnp.dot(dispatch, source, preferred_element_type=jnp.float32).astype(jnp.bfloat16)


def combine(slots, wts, returned, row_slot, first):
    spread = jnp.where(slots[None, :, :] == row_slot[:, None, None], wts[None, :, :], 0.0).sum(axis=2).T
    zero = jnp.zeros_like(spread)
    weights = jnp.concatenate([jnp.where(first[None, :], spread, zero), jnp.where(first[None, :], zero, spread)], axis=0)
    parts = jnp.concatenate(split_three(weights), axis=0)
    summed = jnp.dot(parts, returned, preferred_element_type=jnp.float32)
    return summed.reshape(3, weights.shape[0], returned.shape[1]).sum(axis=0)


def unpack(received, main, tail):
    group_size, _, width = received.shape
    inputs = [received[:, :main].reshape(group_size * main, width)]
    upstream = [received[:, main:2 * main].reshape(group_size * main, width)]
    if tail:
        ends = received[:, 2 * main:].reshape(group_size, 2, tail, width)
        inputs.append(ends[:, 0].reshape(group_size * tail, width))
        upstream.append(ends[:, 1].reshape(group_size * tail, width))
    return inputs, upstream


def repack(result, grads, group_size, main, tail):
    width = result.shape[1]
    edge = group_size * main
    pieces = [result[:edge].reshape(group_size, main, width), grads[:edge].reshape(group_size, main, width)]
    if tail:
        pieces += [result[edge:].reshape(group_size, tail, width), grads[edge:].reshape(group_size, tail, width)]
    return jnp.concatenate(pieces, axis=1)


def per_device(tokens, grad_out, expert_ids, combine_w, w_gate, w_up, w_down):
    token_count, width = tokens.shape
    top_count = expert_ids.shape[1]
    halves = lax.axis_size("half")
    subs = lax.axis_size("sub")
    group_size = lax.axis_size("node") * subs
    experts = group_size * halves
    capacity = max(2, (5 * token_count * top_count + 4 * experts - 1) // (4 * experts))
    slots_per = (capacity + 3) // 4 * 4
    main = slots_per // 8 * 8
    tail = slots_per - main
    row_slot, first = chunk_rows(group_size, slots_per)
    swap = [(i, (i + 1) % halves) for i in range(halves)]
    here = lax.axis_index("half")
    far_stacked = lax.ppermute(jnp.concatenate([tokens, grad_out], axis=0), "half", swap)
    far_ids = lax.ppermute(expert_ids, "half", swap)
    far_w = lax.ppermute(combine_w, "half", swap)

    def near_slots(ids):
        near = (ids % (halves * subs)) // subs == here
        group = (ids // (halves * subs)) * subs + ids % subs
        return route(ids, near, group, group_size, slots_per)

    own_slots = near_slots(expert_ids)
    far_slots = near_slots(far_ids)
    own_sent = inward(pack(own_slots, tokens, grad_out, row_slot, first).reshape(group_size, 2 * slots_per, width))
    far_sent = pack(far_slots, far_stacked[:token_count], far_stacked[token_count:], row_slot, first)
    far_sent = inward(far_sent.reshape(group_size, 2 * slots_per, width))
    own_in, own_up = unpack(own_sent, main, tail)
    far_in, far_up = unpack(far_sent, main, tail)
    result, grads = expert_rows(jnp.concatenate(own_in + far_in, axis=0), jnp.concatenate(own_up + far_up, axis=0),
                                w_gate[0], w_up[0], w_down[0])
    half_rows = group_size * slots_per
    far_back = inward(repack(result[half_rows:], grads[half_rows:], group_size, main, tail))
    far_sum = combine(far_slots, far_w, far_back.reshape(2 * half_rows, width), row_slot, first)
    near_part = lax.ppermute(far_sum.astype(jnp.bfloat16), "half", swap).astype(jnp.float32)
    own_back = inward(repack(result[:half_rows], grads[:half_rows], group_size, main, tail))
    own_sum = combine(own_slots, combine_w, own_back.reshape(2 * half_rows, width), row_slot, first) + near_part
    return (own_sum[:token_count].astype(jnp.bfloat16), own_sum[token_count:].astype(jnp.bfloat16))


def solution(mesh):
    nodes = mesh.shape["node"]
    locals_ = mesh.shape["local"]
    grid = jax.sharding.Mesh(mesh.devices.reshape(nodes, 2, locals_ // 2), ("node", "half", "sub"))
    rows = P(("node", "half", "sub"), None)
    stack = P(("node", "half", "sub"), None, None)
    return jax.shard_map(
        per_device,
        mesh=grid,
        in_specs=(rows, rows, rows, rows, stack, stack, stack),
        out_specs=(rows, rows),
        check_vma=False,
    )
```

```python
import jax
import jax.numpy as jnp
from jax import lax
from jax.sharding import PartitionSpec as P


def expert_rows(inputs, upstream, gate_w, up_w, down_w):
    gate = jnp.dot(inputs, gate_w, preferred_element_type=jnp.float32)
    lifted = jnp.dot(inputs, up_w, preferred_element_type=jnp.float32)
    sigma = jax.nn.sigmoid(gate)
    active = (gate * sigma * lifted).astype(jnp.bfloat16)
    result = jnp.dot(active, down_w, preferred_element_type=jnp.float32).astype(jnp.bfloat16)
    contract = (((1,), (1,)), ((), ()))
    back = lax.dot_general(upstream, down_w, contract, preferred_element_type=jnp.float32)
    d_gate = (back * lifted * sigma * (1.0 + gate * (1.0 - sigma))).astype(jnp.bfloat16)
    d_lift = (back * gate * sigma).astype(jnp.bfloat16)
    grads = lax.dot_general(d_gate, gate_w, contract, preferred_element_type=jnp.float32)
    grads = grads + lax.dot_general(d_lift, up_w, contract, preferred_element_type=jnp.float32)
    return result, grads.astype(jnp.bfloat16)


def row_slots(expert_ids, experts, capacity):
    flat_ids = expert_ids.reshape(-1)
    onehot = (flat_ids[:, None] == jnp.arange(experts, dtype=jnp.int32)[None, :]).astype(jnp.int32)
    ranks = jnp.sum((jnp.cumsum(onehot, axis=0) - 1) * onehot, axis=1)
    return flat_ids * capacity + ranks


def inward(buffer):
    return lax.all_to_all(buffer, ("node", "sub"), split_axis=0, concat_axis=0, tiled=True)


def split_three(weights):
    high = lax.reduce_precision(weights, exponent_bits=8, mantissa_bits=7)
    rest = weights - high
    middle = lax.reduce_precision(rest, exponent_bits=8, mantissa_bits=7)
    low = rest - middle
    return [part.astype(jnp.bfloat16) for part in (high, middle, low)]


def chunk_rows(group_size, slots_per):
    main = slots_per // 8 * 8
    tail = slots_per - main
    place = jnp.arange(2 * slots_per, dtype=jnp.int32)
    in_tail = place >= 2 * main
    rank = jnp.where(in_tail, main + (place - 2 * main) % max(tail, 1), place % max(main, 1))
    part = jnp.where(in_tail, (place - 2 * main) // max(tail, 1), place // max(main, 1))
    row_slot = (jnp.arange(group_size, dtype=jnp.int32)[:, None] * slots_per + rank[None, :]).reshape(-1)
    return row_slot, jnp.tile(part, group_size) == 0


def route(ids, near, group, group_size, slots_per):
    flat = jnp.where(near, group, group_size).reshape(-1)
    onehot = (flat[:, None] == jnp.arange(group_size, dtype=jnp.int32)[None, :]).astype(jnp.int32)
    ranks = jnp.sum((jnp.cumsum(onehot, axis=0) - 1) * onehot, axis=1)
    return jnp.where(flat < group_size, flat * slots_per + ranks, -1).reshape(ids.shape)


def pack(slots, inputs, upstream, row_slot, first):
    hits = slots[None, :, :] == row_slot[:, None, None]
    taken = jnp.any(hits, axis=2).astype(jnp.bfloat16)
    blank = jnp.zeros_like(taken)
    dispatch = jnp.concatenate([jnp.where(first[:, None], taken, blank), jnp.where(first[:, None], blank, taken)], axis=1)
    source = jnp.concatenate([inputs, upstream], axis=0)
    return jnp.dot(dispatch, source, preferred_element_type=jnp.float32).astype(jnp.bfloat16)


def combine(slots, wts, returned, row_slot, first):
    spread = jnp.where(slots[None, :, :] == row_slot[:, None, None], wts[None, :, :], 0.0).sum(axis=2).T
    zero = jnp.zeros_like(spread)
    weights = jnp.concatenate([jnp.where(first[None, :], spread, zero), jnp.where(first[None, :], zero, spread)], axis=0)
    parts = jnp.concatenate(split_three(weights), axis=0)
    summed = jnp.dot(parts, returned, preferred_element_type=jnp.float32)
    return summed.reshape(3, weights.shape[0], returned.shape[1]).sum(axis=0)


def unpack(received, main, tail):
    group_size, _, width = received.shape
    inputs = [received[:, :main].reshape(group_size * main, width)]
    upstream = [received[:, main:2 * main].reshape(group_size * main, width)]
    if tail:
        ends = received[:, 2 * main:].reshape(group_size, 2, tail, width)
        inputs.append(ends[:, 0].reshape(group_size * tail, width))
        upstream.append(ends[:, 1].reshape(group_size * tail, width))
    return inputs, upstream


def repack(result, grads, group_size, main, tail):
    width = result.shape[1]
    edge = group_size * main
    pieces = [result[:edge].reshape(group_size, main, width), grads[:edge].reshape(group_size, main, width)]
    if tail:
        pieces += [result[edge:].reshape(group_size, tail, width), grads[edge:].reshape(group_size, tail, width)]
    return jnp.concatenate(pieces, axis=1)


def per_device(tokens, grad_out, expert_ids, combine_w, w_gate, w_up, w_down):
    token_count, width = tokens.shape
    top_count = expert_ids.shape[1]
    halves = lax.axis_size("half")
    subs = lax.axis_size("sub")
    group_size = lax.axis_size("node") * subs
    experts = group_size * halves
    capacity = max(2, (5 * token_count * top_count + 4 * experts - 1) // (4 * experts))
    slots_per = (capacity + 3) // 4 * 4
    main = slots_per // 8 * 8
    tail = slots_per - main
    row_slot, first = chunk_rows(group_size, slots_per)
    swap = [(i, (i + 1) % halves) for i in range(halves)]
    here = lax.axis_index("half")
    far_stacked = lax.ppermute(jnp.concatenate([tokens, grad_out], axis=0), "half", swap)
    far_ids = lax.ppermute(expert_ids, "half", swap)
    far_w = lax.ppermute(combine_w, "half", swap)

    def near_slots(ids):
        near = (ids % (halves * subs)) // subs == here
        group = (ids // (halves * subs)) * subs + ids % subs
        return route(ids, near, group, group_size, slots_per)

    own_slots = near_slots(expert_ids)
    far_slots = near_slots(far_ids)
    own_sent = inward(pack(own_slots, tokens, grad_out, row_slot, first).reshape(group_size, 2 * slots_per, width))
    far_stacked, far_w, own_sent = lax.optimization_barrier((far_stacked, far_w, own_sent))
    far_sent = pack(far_slots, far_stacked[:token_count], far_stacked[token_count:], row_slot, first)
    far_sent = inward(far_sent.reshape(group_size, 2 * slots_per, width))
    own_in, own_up = unpack(own_sent, main, tail)
    own_res, own_grads = expert_rows(jnp.concatenate(own_in, axis=0), jnp.concatenate(own_up, axis=0),
                                     w_gate[0], w_up[0], w_down[0])
    own_packed = repack(own_res, own_grads, group_size, main, tail)
    far_in, far_up = unpack(far_sent, main, tail)
    far_res, far_grads = expert_rows(jnp.concatenate(far_in, axis=0), jnp.concatenate(far_up, axis=0),
                                     w_gate[0], w_up[0], w_down[0])
    half_rows = group_size * slots_per
    far_back = inward(repack(far_res, far_grads, group_size, main, tail))
    far_sum = combine(far_slots, far_w, far_back.reshape(2 * half_rows, width), row_slot, first).astype(jnp.bfloat16)
    far_sum, own_packed = lax.optimization_barrier((far_sum, own_packed))
    near_part = lax.ppermute(far_sum, "half", swap).astype(jnp.float32)
    own_back = inward(own_packed)
    own_sum = combine(own_slots, combine_w, own_back.reshape(2 * half_rows, width), row_slot, first) + near_part
    return (own_sum[:token_count].astype(jnp.bfloat16), own_sum[token_count:].astype(jnp.bfloat16))


def solution(mesh):
    nodes = mesh.shape["node"]
    locals_ = mesh.shape["local"]
    grid = jax.sharding.Mesh(mesh.devices.reshape(nodes, 2, locals_ // 2), ("node", "half", "sub"))
    rows = P(("node", "half", "sub"), None)
    stack = P(("node", "half", "sub"), None, None)
    return jax.shard_map(
        per_device,
        mesh=grid,
        in_specs=(rows, rows, rows, rows, stack, stack, stack),
        out_specs=(rows, rows),
        check_vma=False,
    )
```

```python
import jax
import jax.numpy as jnp
from jax import lax
from jax.sharding import PartitionSpec as P


def expert_rows(inputs, upstream, gate_w, up_w, down_w):
    gate = jnp.dot(inputs, gate_w, preferred_element_type=jnp.float32)
    lifted = jnp.dot(inputs, up_w, preferred_element_type=jnp.float32)
    sigma = jax.nn.sigmoid(gate)
    active = (gate * sigma * lifted).astype(jnp.bfloat16)
    result = jnp.dot(active, down_w, preferred_element_type=jnp.float32).astype(jnp.bfloat16)
    contract = (((1,), (1,)), ((), ()))
    back = lax.dot_general(upstream, down_w, contract, preferred_element_type=jnp.float32)
    d_gate = (back * lifted * sigma * (1.0 + gate * (1.0 - sigma))).astype(jnp.bfloat16)
    d_lift = (back * gate * sigma).astype(jnp.bfloat16)
    grads = lax.dot_general(d_gate, gate_w, contract, preferred_element_type=jnp.float32)
    grads = grads + lax.dot_general(d_lift, up_w, contract, preferred_element_type=jnp.float32)
    return result, grads.astype(jnp.bfloat16)


def row_slots(expert_ids, experts, capacity):
    flat_ids = expert_ids.reshape(-1)
    onehot = (flat_ids[:, None] == jnp.arange(experts, dtype=jnp.int32)[None, :]).astype(jnp.int32)
    ranks = jnp.sum((jnp.cumsum(onehot, axis=0) - 1) * onehot, axis=1)
    return flat_ids * capacity + ranks


def inward(buffer):
    return lax.all_to_all(buffer, ("node", "sub"), split_axis=0, concat_axis=0, tiled=True)


def split_three(weights):
    high = lax.reduce_precision(weights, exponent_bits=8, mantissa_bits=7)
    rest = weights - high
    middle = lax.reduce_precision(rest, exponent_bits=8, mantissa_bits=7)
    low = rest - middle
    return [part.astype(jnp.bfloat16) for part in (high, middle, low)]


def chunk_rows(group_size, slots_per):
    main = slots_per // 8 * 8
    tail = slots_per - main
    place = jnp.arange(2 * slots_per, dtype=jnp.int32)
    in_tail = place >= 2 * main
    rank = jnp.where(in_tail, main + (place - 2 * main) % max(tail, 1), place % max(main, 1))
    part = jnp.where(in_tail, (place - 2 * main) // max(tail, 1), place // max(main, 1))
    row_slot = (jnp.arange(group_size, dtype=jnp.int32)[:, None] * slots_per + rank[None, :]).reshape(-1)
    return row_slot, jnp.tile(part, group_size) == 0


def route(ids, near, group, group_size, slots_per):
    flat = jnp.where(near, group, group_size).reshape(-1)
    onehot = (flat[:, None] == jnp.arange(group_size, dtype=jnp.int32)[None, :]).astype(jnp.int32)
    ranks = jnp.sum((jnp.cumsum(onehot, axis=0) - 1) * onehot, axis=1)
    return jnp.where(flat < group_size, flat * slots_per + ranks, -1).reshape(ids.shape)


def pack(slots, inputs, upstream, row_slot, first):
    hits = slots[None, :, :] == row_slot[:, None, None]
    taken = jnp.any(hits, axis=2).astype(jnp.bfloat16)
    blank = jnp.zeros_like(taken)
    dispatch = jnp.concatenate([jnp.where(first[:, None], taken, blank), jnp.where(first[:, None], blank, taken)], axis=1)
    source = jnp.concatenate([inputs, upstream], axis=0)
    return jnp.dot(dispatch, source, preferred_element_type=jnp.float32).astype(jnp.bfloat16)


def combine(slots, wts, returned, row_slot, first):
    spread = jnp.where(slots[None, :, :] == row_slot[:, None, None], wts[None, :, :], 0.0).sum(axis=2).T
    zero = jnp.zeros_like(spread)
    weights = jnp.concatenate([jnp.where(first[None, :], spread, zero), jnp.where(first[None, :], zero, spread)], axis=0)
    parts = jnp.concatenate(split_three(weights), axis=0)
    summed = jnp.dot(parts, returned, preferred_element_type=jnp.float32)
    return summed.reshape(3, weights.shape[0], returned.shape[1]).sum(axis=0)


def unpack(received, main, tail):
    group_size, _, width = received.shape
    inputs = [received[:, :main].reshape(group_size * main, width)]
    upstream = [received[:, main:2 * main].reshape(group_size * main, width)]
    if tail:
        ends = received[:, 2 * main:].reshape(group_size, 2, tail, width)
        inputs.append(ends[:, 0].reshape(group_size * tail, width))
        upstream.append(ends[:, 1].reshape(group_size * tail, width))
    return inputs, upstream


def repack(result, grads, group_size, main, tail):
    width = result.shape[1]
    edge = group_size * main
    pieces = [result[:edge].reshape(group_size, main, width), grads[:edge].reshape(group_size, main, width)]
    if tail:
        pieces += [result[edge:].reshape(group_size, tail, width), grads[edge:].reshape(group_size, tail, width)]
    return jnp.concatenate(pieces, axis=1)


def expert_split(inputs, upstream, gate_w, up_w, down_w):
    bounds = []
    edge = 0
    for piece in inputs:
        bounds.append((edge, edge + piece.shape[1]))
        edge += piece.shape[1]
    contract = (((1,), (1,)), ((), ()))
    gate = sum(jnp.dot(x, gate_w[a:b], preferred_element_type=jnp.float32) for x, (a, b) in zip(inputs, bounds))
    lifted = sum(jnp.dot(x, up_w[a:b], preferred_element_type=jnp.float32) for x, (a, b) in zip(inputs, bounds))
    back = sum(lax.dot_general(g, down_w[:, a:b], contract, preferred_element_type=jnp.float32) for g, (a, b) in zip(upstream, bounds))
    sigma = jax.nn.sigmoid(gate)
    active = (gate * sigma * lifted).astype(jnp.bfloat16)
    d_gate = (back * lifted * sigma * (1.0 + gate * (1.0 - sigma))).astype(jnp.bfloat16)
    d_lift = (back * gate * sigma).astype(jnp.bfloat16)
    results, grads = [], []
    for a, b in bounds:
        results.append(jnp.dot(active, down_w[:, a:b], preferred_element_type=jnp.float32).astype(jnp.bfloat16))
        total = lax.dot_general(d_gate, gate_w[a:b], contract, preferred_element_type=jnp.float32)
        total = total + lax.dot_general(d_lift, up_w[a:b], contract, preferred_element_type=jnp.float32)
        grads.append(total.astype(jnp.bfloat16))
    return results, grads


def per_device(tokens, grad_out, expert_ids, combine_w, w_gate, w_up, w_down):
    token_count, width = tokens.shape
    top_count = expert_ids.shape[1]
    halves = lax.axis_size("half")
    subs = lax.axis_size("sub")
    group_size = lax.axis_size("node") * subs
    experts = group_size * halves
    capacity = max(2, (5 * token_count * top_count + 4 * experts - 1) // (4 * experts))
    slots_per = (capacity + 3) // 4 * 4
    main = slots_per // 8 * 8
    tail = slots_per - main
    half_rows = group_size * slots_per
    row_slot, first = chunk_rows(group_size, slots_per)
    swap = [(i, (i + 1) % halves) for i in range(halves)]
    here = lax.axis_index("half")
    cut = width // 2
    far_lo = lax.ppermute(jnp.concatenate([tokens[:, :cut], grad_out[:, :cut]], axis=0), "half", swap)
    far_hi = lax.ppermute(jnp.concatenate([tokens[:, cut:], grad_out[:, cut:]], axis=0), "half", swap)
    far_ids = lax.ppermute(expert_ids, "half", swap)
    far_w = lax.ppermute(combine_w, "half", swap)

    def near_slots(ids):
        near = (ids % (halves * subs)) // subs == here
        group = (ids // (halves * subs)) * subs + ids % subs
        return route(ids, near, group, group_size, slots_per)

    own_slots = near_slots(expert_ids)
    far_slots = near_slots(far_ids)
    own_sent = inward(pack(own_slots, tokens, grad_out, row_slot, first).reshape(group_size, 2 * slots_per, width))
    far_lo, far_w, own_sent = lax.optimization_barrier((far_lo, far_w, own_sent))
    lo_sent = pack(far_slots, far_lo[:token_count], far_lo[token_count:], row_slot, first)
    lo_sent = inward(lo_sent.reshape(group_size, 2 * slots_per, cut))
    far_hi, lo_sent = lax.optimization_barrier((far_hi, lo_sent))
    hi_sent = pack(far_slots, far_hi[:token_count], far_hi[token_count:], row_slot, first)
    hi_sent = inward(hi_sent.reshape(group_size, 2 * slots_per, width - cut))
    own_in, own_up = unpack(own_sent, main, tail)
    own_res, own_grads = expert_split([jnp.concatenate(own_in, axis=0)], [jnp.concatenate(own_up, axis=0)],
                                      w_gate[0], w_up[0], w_down[0])
    own_packed = repack(own_res[0], own_grads[0], group_size, main, tail)
    lo_in, lo_up = unpack(lo_sent, main, tail)
    hi_in, hi_up = unpack(hi_sent, main, tail)
    far_res, far_grads = expert_split([jnp.concatenate(lo_in, axis=0), jnp.concatenate(hi_in, axis=0)],
                                      [jnp.concatenate(lo_up, axis=0), jnp.concatenate(hi_up, axis=0)],
                                      w_gate[0], w_up[0], w_down[0])
    lo_back = inward(repack(far_res[0], far_grads[0], group_size, main, tail))
    lo_sum = combine(far_slots, far_w, lo_back.reshape(2 * half_rows, cut), row_slot, first).astype(jnp.bfloat16)
    near_lo = lax.ppermute(lo_sum, "half", swap)
    hi_back = inward(repack(far_res[1], far_grads[1], group_size, main, tail))
    near_lo, hi_back = lax.optimization_barrier((near_lo, hi_back))
    hi_sum = combine(far_slots, far_w, hi_back.reshape(2 * half_rows, width - cut), row_slot, first).astype(jnp.bfloat16)
    near_hi = lax.ppermute(hi_sum, "half", swap)
    near_parts = [near_lo, near_hi]
    sums = [lo_sum, hi_sum]
    last, own_packed = lax.optimization_barrier((sums[-1], own_packed))
    own_back = inward(own_packed)
    near_part = jnp.concatenate(near_parts, axis=1).astype(jnp.float32)
    own_sum = combine(own_slots, combine_w, own_back.reshape(2 * half_rows, width), row_slot, first) + near_part
    return (own_sum[:token_count].astype(jnp.bfloat16), own_sum[token_count:].astype(jnp.bfloat16))


def solution(mesh):
    nodes = mesh.shape["node"]
    locals_ = mesh.shape["local"]
    grid = jax.sharding.Mesh(mesh.devices.reshape(nodes, 2, locals_ // 2), ("node", "half", "sub"))
    rows = P(("node", "half", "sub"), None)
    stack = P(("node", "half", "sub"), None, None)
    return jax.shard_map(
        per_device,
        mesh=grid,
        in_specs=(rows, rows, rows, rows, stack, stack, stack),
        out_specs=(rows, rows),
        check_vma=False,
    )
```

```python
import jax
import jax.numpy as jnp
from jax import lax
from jax.sharding import PartitionSpec as P


def expert_rows(inputs, upstream, gate_w, up_w, down_w, edge):
    gate = jnp.dot(inputs, gate_w, preferred_element_type=jnp.float32)
    lifted = jnp.dot(inputs, up_w, preferred_element_type=jnp.float32)
    sigma = jax.nn.sigmoid(gate)
    active = (gate * sigma * lifted).astype(jnp.bfloat16)
    contract = (((1,), (1,)), ((), ()))
    back = lax.dot_general(upstream, down_w, contract, preferred_element_type=jnp.float32)
    d_gate = (back * lifted * sigma * (1.0 + gate * (1.0 - sigma))).astype(jnp.bfloat16)
    d_lift = (back * gate * sigma).astype(jnp.bfloat16)
    results, grads = [], []
    for rows in (slice(0, edge), slice(edge, inputs.shape[0])):
        if rows.stop > rows.start:
            results.append(jnp.dot(active[rows], down_w, preferred_element_type=jnp.float32).astype(jnp.bfloat16))
            total = lax.dot_general(d_gate[rows], gate_w, contract, preferred_element_type=jnp.float32)
            total = total + lax.dot_general(d_lift[rows], up_w, contract, preferred_element_type=jnp.float32)
            grads.append(total.astype(jnp.bfloat16))
    return results, grads


def row_slots(expert_ids, experts, capacity):
    flat_ids = expert_ids.reshape(-1)
    onehot = (flat_ids[:, None] == jnp.arange(experts, dtype=jnp.int32)[None, :]).astype(jnp.int32)
    ranks = jnp.sum((jnp.cumsum(onehot, axis=0) - 1) * onehot, axis=1)
    return flat_ids * capacity + ranks


def inward(buffer):
    return lax.all_to_all(buffer, ("node", "sub"), split_axis=0, concat_axis=0, tiled=True)


def split_three(weights):
    high = lax.reduce_precision(weights, exponent_bits=8, mantissa_bits=7)
    rest = weights - high
    middle = lax.reduce_precision(rest, exponent_bits=8, mantissa_bits=7)
    low = rest - middle
    return [part.astype(jnp.bfloat16) for part in (high, middle, low)]


def chunk_rows(group_size, slots_per):
    main = slots_per // 8 * 8
    tail = slots_per - main
    place = jnp.arange(2 * slots_per, dtype=jnp.int32)
    in_tail = place >= 2 * main
    rank = jnp.where(in_tail, main + (place - 2 * main) % max(tail, 1), place % max(main, 1))
    part = jnp.where(in_tail, (place - 2 * main) // max(tail, 1), place // max(main, 1))
    row_slot = (jnp.arange(group_size, dtype=jnp.int32)[:, None] * slots_per + rank[None, :]).reshape(-1)
    return row_slot, jnp.tile(part, group_size) == 0


def route(ids, near, group, group_size, slots_per):
    flat = jnp.where(near, group, group_size).reshape(-1)
    onehot = (flat[:, None] == jnp.arange(group_size, dtype=jnp.int32)[None, :]).astype(jnp.int32)
    ranks = jnp.sum((jnp.cumsum(onehot, axis=0) - 1) * onehot, axis=1)
    return jnp.where(flat < group_size, flat * slots_per + ranks, -1).reshape(ids.shape)


def pack(slots, inputs, upstream, row_slot, first):
    hits = slots[None, :, :] == row_slot[:, None, None]
    taken = jnp.any(hits, axis=2).astype(jnp.bfloat16)
    blank = jnp.zeros_like(taken)
    dispatch = jnp.concatenate([jnp.where(first[:, None], taken, blank), jnp.where(first[:, None], blank, taken)], axis=1)
    source = jnp.concatenate([inputs, upstream], axis=0)
    return jnp.dot(dispatch, source, preferred_element_type=jnp.float32).astype(jnp.bfloat16)


def combine(slots, wts, returned, row_slot, first):
    spread = jnp.where(slots[None, :, :] == row_slot[:, None, None], wts[None, :, :], 0.0).sum(axis=2).T
    zero = jnp.zeros_like(spread)
    weights = jnp.concatenate([jnp.where(first[None, :], spread, zero), jnp.where(first[None, :], zero, spread)], axis=0)
    parts = jnp.concatenate(split_three(weights), axis=0)
    summed = jnp.dot(parts, returned, preferred_element_type=jnp.float32)
    return summed.reshape(3, weights.shape[0], returned.shape[1]).sum(axis=0)


def unpack(received, main, tail):
    group_size, _, width = received.shape
    inputs = [received[:, :main].reshape(group_size * main, width)]
    upstream = [received[:, main:2 * main].reshape(group_size * main, width)]
    if tail:
        ends = received[:, 2 * main:].reshape(group_size, 2, tail, width)
        inputs.append(ends[:, 0].reshape(group_size * tail, width))
        upstream.append(ends[:, 1].reshape(group_size * tail, width))
    return inputs, upstream


def repack(results, grads, group_size, main, tail):
    width = results[0].shape[1]
    pieces = [results[0].reshape(group_size, main, width), grads[0].reshape(group_size, main, width)]
    if tail:
        pieces += [results[1].reshape(group_size, tail, width), grads[1].reshape(group_size, tail, width)]
    return jnp.concatenate(pieces, axis=1)


def per_device(tokens, grad_out, expert_ids, combine_w, w_gate, w_up, w_down):
    token_count, width = tokens.shape
    top_count = expert_ids.shape[1]
    halves = lax.axis_size("half")
    subs = lax.axis_size("sub")
    group_size = lax.axis_size("node") * subs
    experts = group_size * halves
    capacity = max(2, (5 * token_count * top_count + 4 * experts - 1) // (4 * experts))
    slots_per = (capacity + 3) // 4 * 4
    main = slots_per // 8 * 8
    tail = slots_per - main
    row_slot, first = chunk_rows(group_size, slots_per)
    swap = [(i, (i + 1) % halves) for i in range(halves)]
    here = lax.axis_index("half")
    count = token_count * top_count
    meta_rows = -(-4 * count // width)
    meta = jnp.concatenate([expert_ids.reshape(-1).astype(jnp.bfloat16)] + [p.reshape(-1) for p in split_three(combine_w)])
    meta = jnp.pad(meta, (0, meta_rows * width - 4 * count)).reshape(meta_rows, width)
    meta = jnp.pad(meta, ((0, (-meta_rows) % 8), (0, 0)))
    far_all = lax.ppermute(jnp.concatenate([tokens, grad_out, meta], axis=0), "half", swap)

    def near_slots(ids):
        near = (ids % (halves * subs)) // subs == here
        group = (ids // (halves * subs)) * subs + ids % subs
        return route(ids, near, group, group_size, slots_per)

    own_slots = near_slots(expert_ids)
    own_sent = inward(pack(own_slots, tokens, grad_out, row_slot, first).reshape(group_size, 2 * slots_per, width))
    far_all, own_sent = lax.optimization_barrier((far_all, own_sent))
    far_stacked = far_all[:2 * token_count]
    far_meta = far_all[2 * token_count:].reshape(-1)[:4 * count].astype(jnp.float32)
    far_ids = far_meta[:count].astype(jnp.int32).reshape(token_count, top_count)
    far_w = (far_meta[count:2 * count] + far_meta[2 * count:3 * count] + far_meta[3 * count:]).reshape(token_count, top_count)
    far_slots = near_slots(far_ids)
    far_sent = pack(far_slots, far_stacked[:token_count], far_stacked[token_count:], row_slot, first)
    far_sent = inward(far_sent.reshape(group_size, 2 * slots_per, width))
    own_in, own_up = unpack(own_sent, main, tail)
    own_res, own_grads = expert_rows(jnp.concatenate(own_in, axis=0), jnp.concatenate(own_up, axis=0),
                                     w_gate[0], w_up[0], w_down[0], group_size * main)
    own_packed = repack(own_res, own_grads, group_size, main, tail)
    far_in, far_up = unpack(far_sent, main, tail)
    far_res, far_grads = expert_rows(jnp.concatenate(far_in, axis=0), jnp.concatenate(far_up, axis=0),
                                     w_gate[0], w_up[0], w_down[0], group_size * main)
    half_rows = group_size * slots_per
    far_back = inward(repack(far_res, far_grads, group_size, main, tail))
    far_sum = combine(far_slots, far_w, far_back.reshape(2 * half_rows, width), row_slot, first).astype(jnp.bfloat16)
    far_sum, own_packed = lax.optimization_barrier((far_sum, own_packed))
    near_part = lax.ppermute(far_sum, "half", swap).astype(jnp.float32)
    own_back = inward(own_packed)
    own_sum = combine(own_slots, combine_w, own_back.reshape(2 * half_rows, width), row_slot, first) + near_part
    return (own_sum[:token_count].astype(jnp.bfloat16), own_sum[token_count:].astype(jnp.bfloat16))


def solution(mesh):
    nodes = mesh.shape["node"]
    locals_ = mesh.shape["local"]
    grid = jax.sharding.Mesh(mesh.devices.reshape(nodes, 2, locals_ // 2), ("node", "half", "sub"))
    rows = P(("node", "half", "sub"), None)
    stack = P(("node", "half", "sub"), None, None)
    return jax.shard_map(
        per_device,
        mesh=grid,
        in_specs=(rows, rows, rows, rows, stack, stack, stack),
        out_specs=(rows, rows),
        check_vma=False,
    )
```

```python
import jax
import jax.numpy as jnp
from jax import lax
from jax.sharding import PartitionSpec as P


def expert_rows(inputs, upstream, gate_w, up_w, down_w):
    gate = jnp.dot(inputs, gate_w, preferred_element_type=jnp.float32)
    lifted = jnp.dot(inputs, up_w, preferred_element_type=jnp.float32)
    sigma = jax.nn.sigmoid(gate)
    active = (gate * sigma * lifted).astype(jnp.bfloat16)
    result = jnp.dot(active, down_w, preferred_element_type=jnp.float32).astype(jnp.bfloat16)
    contract = (((1,), (1,)), ((), ()))
    back = lax.dot_general(upstream, down_w, contract, preferred_element_type=jnp.float32)
    d_gate = (back * lifted * sigma * (1.0 + gate * (1.0 - sigma))).astype(jnp.bfloat16)
    d_lift = (back * gate * sigma).astype(jnp.bfloat16)
    grads = lax.dot_general(d_gate, gate_w, contract, preferred_element_type=jnp.float32)
    grads = grads + lax.dot_general(d_lift, up_w, contract, preferred_element_type=jnp.float32)
    return result, grads.astype(jnp.bfloat16)


def row_slots(expert_ids, experts, capacity):
    flat_ids = expert_ids.reshape(-1)
    onehot = (flat_ids[:, None] == jnp.arange(experts, dtype=jnp.int32)[None, :]).astype(jnp.int32)
    ranks = jnp.sum((jnp.cumsum(onehot, axis=0) - 1) * onehot, axis=1)
    return flat_ids * capacity + ranks


def inward(buffer):
    return lax.all_to_all(buffer, ("node", "sub"), split_axis=0, concat_axis=0, tiled=True)


def split_three(weights):
    high = lax.reduce_precision(weights, exponent_bits=8, mantissa_bits=7)
    rest = weights - high
    middle = lax.reduce_precision(rest, exponent_bits=8, mantissa_bits=7)
    low = rest - middle
    return [part.astype(jnp.bfloat16) for part in (high, middle, low)]


def chunk_rows(group_size, slots_per):
    main = slots_per // 8 * 8
    tail = slots_per - main
    place = jnp.arange(2 * slots_per, dtype=jnp.int32)
    in_tail = place >= 2 * main
    rank = jnp.where(in_tail, main + (place - 2 * main) % max(tail, 1), place % max(main, 1))
    part = jnp.where(in_tail, (place - 2 * main) // max(tail, 1), place // max(main, 1))
    row_slot = (jnp.arange(group_size, dtype=jnp.int32)[:, None] * slots_per + rank[None, :]).reshape(-1)
    return row_slot, jnp.tile(part, group_size) == 0


def route(ids, near, group, group_size, slots_per):
    flat = jnp.where(near, group, group_size).reshape(-1)
    onehot = (flat[:, None] == jnp.arange(group_size, dtype=jnp.int32)[None, :]).astype(jnp.int32)
    ranks = jnp.sum((jnp.cumsum(onehot, axis=0) - 1) * onehot, axis=1)
    return jnp.where(flat < group_size, flat * slots_per + ranks, -1).reshape(ids.shape)


def pack(slots, inputs, upstream, row_slot, first):
    hits = slots[None, :, :] == row_slot[:, None, None]
    taken = jnp.any(hits, axis=2).astype(jnp.bfloat16)
    blank = jnp.zeros_like(taken)
    dispatch = jnp.concatenate([jnp.where(first[:, None], taken, blank), jnp.where(first[:, None], blank, taken)], axis=1)
    source = jnp.concatenate([inputs, upstream], axis=0)
    return jnp.dot(dispatch, source, preferred_element_type=jnp.float32).astype(jnp.bfloat16)


def combine(slots, wts, returned, row_slot, first):
    spread = jnp.where(slots[None, :, :] == row_slot[:, None, None], wts[None, :, :], 0.0).sum(axis=2).T
    zero = jnp.zeros_like(spread)
    weights = jnp.concatenate([jnp.where(first[None, :], spread, zero), jnp.where(first[None, :], zero, spread)], axis=0)
    parts = jnp.concatenate(split_three(weights), axis=0)
    summed = jnp.dot(parts, returned, preferred_element_type=jnp.float32)
    return summed.reshape(3, weights.shape[0], returned.shape[1]).sum(axis=0)


def unpack(received, main, tail):
    group_size, _, width = received.shape
    inputs = [received[:, :main].reshape(group_size * main, width)]
    upstream = [received[:, main:2 * main].reshape(group_size * main, width)]
    if tail:
        ends = received[:, 2 * main:].reshape(group_size, 2, tail, width)
        inputs.append(ends[:, 0].reshape(group_size * tail, width))
        upstream.append(ends[:, 1].reshape(group_size * tail, width))
    return inputs, upstream


def repack(result, grads, group_size, main, tail):
    width = result.shape[1]
    edge = group_size * main
    pieces = [result[:edge].reshape(group_size, main, width), grads[:edge].reshape(group_size, main, width)]
    if tail:
        pieces += [result[edge:].reshape(group_size, tail, width), grads[edge:].reshape(group_size, tail, width)]
    return jnp.concatenate(pieces, axis=1)


def per_device(tokens, grad_out, expert_ids, combine_w, w_gate, w_up, w_down):
    token_count, width = tokens.shape
    top_count = expert_ids.shape[1]
    halves = lax.axis_size("half")
    subs = lax.axis_size("sub")
    group_size = lax.axis_size("node") * subs
    experts = group_size * halves
    capacity = max(2, (5 * token_count * top_count + 4 * experts - 1) // (4 * experts))
    slots_per = (capacity + 3) // 4 * 4
    main = slots_per // 8 * 8
    tail = slots_per - main
    row_slot, first = chunk_rows(group_size, slots_per)
    swap = [(i, (i + 1) % halves) for i in range(halves)]
    here = lax.axis_index("half")
    far_stacked = lax.ppermute(jnp.concatenate([tokens, grad_out], axis=0), "half", swap)
    far_ids = lax.ppermute(expert_ids, "half", swap)
    far_w = lax.ppermute(combine_w, "half", swap)

    def near_slots(ids):
        near = (ids % (halves * subs)) // subs == here
        group = (ids // (halves * subs)) * subs + ids % subs
        return route(ids, near, group, group_size, slots_per)

    own_slots = near_slots(expert_ids)
    far_slots = near_slots(far_ids)
    own_sent = inward(pack(own_slots, tokens, grad_out, row_slot, first).reshape(group_size, 2 * slots_per, width))
    far_stacked, far_w, own_sent = lax.optimization_barrier((far_stacked, far_w, own_sent))
    far_sent = pack(far_slots, far_stacked[:token_count], far_stacked[token_count:], row_slot, first)
    far_sent = inward(far_sent.reshape(group_size, 2 * slots_per, width))
    own_in, own_up = unpack(own_sent, main, tail)
    own_res, own_grads = expert_rows(jnp.concatenate(own_in, axis=0), jnp.concatenate(own_up, axis=0),
                                     w_gate[0], w_up[0], w_down[0])
    own_packed = repack(own_res, own_grads, group_size, main, tail)
    far_in, far_up = unpack(far_sent, main, tail)
    far_res, far_grads = expert_rows(jnp.concatenate(far_in, axis=0), jnp.concatenate(far_up, axis=0),
                                     w_gate[0], w_up[0], w_down[0])
    half_rows = group_size * slots_per
    far_back = inward(repack(far_res, far_grads, group_size, main, tail))
    far_back, own_packed = lax.optimization_barrier((far_back, own_packed))
    far_sum = combine(far_slots, far_w, far_back.reshape(2 * half_rows, width), row_slot, first).astype(jnp.bfloat16)
    near_part = lax.ppermute(far_sum, "half", swap).astype(jnp.float32)
    own_back = inward(own_packed)
    own_sum = combine(own_slots, combine_w, own_back.reshape(2 * half_rows, width), row_slot, first) + near_part
    return (own_sum[:token_count].astype(jnp.bfloat16), own_sum[token_count:].astype(jnp.bfloat16))


def solution(mesh):
    nodes = mesh.shape["node"]
    locals_ = mesh.shape["local"]
    grid = jax.sharding.Mesh(mesh.devices.reshape(nodes, 2, locals_ // 2), ("node", "half", "sub"))
    rows = P(("node", "half", "sub"), None)
    stack = P(("node", "half", "sub"), None, None)
    return jax.shard_map(
        per_device,
        mesh=grid,
        in_specs=(rows, rows, rows, rows, stack, stack, stack),
        out_specs=(rows, rows),
        check_vma=False,
    )
```

```python
import jax
import jax.numpy as jnp
from jax import lax
from jax.sharding import PartitionSpec as P


def expert_rows(inputs, upstream, both_w, down_w):
    ff = down_w.shape[0]
    joint = jnp.dot(inputs, both_w, preferred_element_type=jnp.float32)
    gate = joint[:, :ff]
    lifted = joint[:, ff:]
    sigma = jax.nn.sigmoid(gate)
    active = (gate * sigma * lifted).astype(jnp.bfloat16)
    result = jnp.dot(active, down_w, preferred_element_type=jnp.float32).astype(jnp.bfloat16)
    contract = (((1,), (1,)), ((), ()))
    back = lax.dot_general(upstream, down_w, contract, preferred_element_type=jnp.float32)
    d_gate = (back * lifted * sigma * (1.0 + gate * (1.0 - sigma))).astype(jnp.bfloat16)
    d_lift = (back * gate * sigma).astype(jnp.bfloat16)
    grads = lax.dot_general(jnp.concatenate([d_gate, d_lift], axis=1), both_w, contract, preferred_element_type=jnp.float32)
    return result, grads.astype(jnp.bfloat16)


def row_slots(expert_ids, experts, capacity):
    flat_ids = expert_ids.reshape(-1)
    onehot = (flat_ids[:, None] == jnp.arange(experts, dtype=jnp.int32)[None, :]).astype(jnp.int32)
    ranks = jnp.sum((jnp.cumsum(onehot, axis=0) - 1) * onehot, axis=1)
    return flat_ids * capacity + ranks


def inward(buffer):
    return lax.all_to_all(buffer, ("node", "sub"), split_axis=0, concat_axis=0, tiled=True)


def split_three(weights):
    high = lax.reduce_precision(weights, exponent_bits=8, mantissa_bits=7)
    rest = weights - high
    middle = lax.reduce_precision(rest, exponent_bits=8, mantissa_bits=7)
    low = rest - middle
    return [part.astype(jnp.bfloat16) for part in (high, middle, low)]


def chunk_rows(group_size, slots_per):
    main = slots_per // 8 * 8
    tail = slots_per - main
    place = jnp.arange(2 * slots_per, dtype=jnp.int32)
    in_tail = place >= 2 * main
    rank = jnp.where(in_tail, main + (place - 2 * main) % max(tail, 1), place % max(main, 1))
    part = jnp.where(in_tail, (place - 2 * main) // max(tail, 1), place // max(main, 1))
    row_slot = (jnp.arange(group_size, dtype=jnp.int32)[:, None] * slots_per + rank[None, :]).reshape(-1)
    return row_slot, jnp.tile(part, group_size) == 0


def route(ids, near, group, group_size, slots_per):
    flat = jnp.where(near, group, group_size).reshape(-1)
    onehot = (flat[:, None] == jnp.arange(group_size, dtype=jnp.int32)[None, :]).astype(jnp.int32)
    ranks = jnp.sum((jnp.cumsum(onehot, axis=0) - 1) * onehot, axis=1)
    return jnp.where(flat < group_size, flat * slots_per + ranks, -1).reshape(ids.shape)


def pack(slots, inputs, upstream, row_slot, first):
    hits = slots[None, :, :] == row_slot[:, None, None]
    taken = jnp.any(hits, axis=2).astype(jnp.bfloat16)
    blank = jnp.zeros_like(taken)
    dispatch = jnp.concatenate([jnp.where(first[:, None], taken, blank), jnp.where(first[:, None], blank, taken)], axis=1)
    source = jnp.concatenate([inputs, upstream], axis=0)
    return jnp.dot(dispatch, source, preferred_element_type=jnp.float32).astype(jnp.bfloat16)


def combine(slots, wts, returned, row_slot, first):
    spread = jnp.where(slots[None, :, :] == row_slot[:, None, None], wts[None, :, :], 0.0).sum(axis=2).T
    zero = jnp.zeros_like(spread)
    weights = jnp.concatenate([jnp.where(first[None, :], spread, zero), jnp.where(first[None, :], zero, spread)], axis=0)
    parts = jnp.concatenate(split_three(weights), axis=0)
    summed = jnp.dot(parts, returned, preferred_element_type=jnp.float32)
    return summed.reshape(3, weights.shape[0], returned.shape[1]).sum(axis=0)


def unpack(received, main, tail):
    group_size, _, width = received.shape
    inputs = [received[:, :main].reshape(group_size * main, width)]
    upstream = [received[:, main:2 * main].reshape(group_size * main, width)]
    if tail:
        ends = received[:, 2 * main:].reshape(group_size, 2, tail, width)
        inputs.append(ends[:, 0].reshape(group_size * tail, width))
        upstream.append(ends[:, 1].reshape(group_size * tail, width))
    return inputs, upstream


def repack(result, grads, group_size, main, tail):
    width = result.shape[1]
    edge = group_size * main
    pieces = [result[:edge].reshape(group_size, main, width), grads[:edge].reshape(group_size, main, width)]
    if tail:
        pieces += [result[edge:].reshape(group_size, tail, width), grads[edge:].reshape(group_size, tail, width)]
    return jnp.concatenate(pieces, axis=1)


def per_device(tokens, grad_out, expert_ids, combine_w, w_gate, w_up, w_down):
    token_count, width = tokens.shape
    top_count = expert_ids.shape[1]
    halves = lax.axis_size("half")
    subs = lax.axis_size("sub")
    group_size = lax.axis_size("node") * subs
    experts = group_size * halves
    capacity = max(2, (5 * token_count * top_count + 4 * experts - 1) // (4 * experts))
    slots_per = (capacity + 3) // 4 * 4
    main = slots_per // 8 * 8
    tail = slots_per - main
    row_slot, first = chunk_rows(group_size, slots_per)
    swap = [(i, (i + 1) % halves) for i in range(halves)]
    here = lax.axis_index("half")
    far_stacked = lax.ppermute(jnp.concatenate([tokens, grad_out], axis=0), "half", swap)
    far_ids = lax.ppermute(expert_ids, "half", swap)
    far_w = lax.ppermute(combine_w, "half", swap)

    def near_slots(ids):
        near = (ids % (halves * subs)) // subs == here
        group = (ids // (halves * subs)) * subs + ids % subs
        return route(ids, near, group, group_size, slots_per)

    both_w = jnp.concatenate([w_gate[0], w_up[0]], axis=1)
    own_slots = near_slots(expert_ids)
    far_slots = near_slots(far_ids)
    own_sent = inward(pack(own_slots, tokens, grad_out, row_slot, first).reshape(group_size, 2 * slots_per, width))
    far_stacked, far_w, own_sent = lax.optimization_barrier((far_stacked, far_w, own_sent))
    far_sent = pack(far_slots, far_stacked[:token_count], far_stacked[token_count:], row_slot, first)
    far_sent = inward(far_sent.reshape(group_size, 2 * slots_per, width))
    own_in, own_up = unpack(own_sent, main, tail)
    own_res, own_grads = expert_rows(jnp.concatenate(own_in, axis=0), jnp.concatenate(own_up, axis=0),
                                     both_w, w_down[0])
    own_packed = repack(own_res, own_grads, group_size, main, tail)
    far_in, far_up = unpack(far_sent, main, tail)
    far_res, far_grads = expert_rows(jnp.concatenate(far_in, axis=0), jnp.concatenate(far_up, axis=0),
                                     both_w, w_down[0])
    half_rows = group_size * slots_per
    far_back = inward(repack(far_res, far_grads, group_size, main, tail))
    far_back, own_packed = lax.optimization_barrier((far_back, own_packed))
    far_sum = combine(far_slots, far_w, far_back.reshape(2 * half_rows, width), row_slot, first).astype(jnp.bfloat16)
    near_part = lax.ppermute(far_sum, "half", swap).astype(jnp.float32)
    own_back = inward(own_packed)
    own_sum = combine(own_slots, combine_w, own_back.reshape(2 * half_rows, width), row_slot, first) + near_part
    return (own_sum[:token_count].astype(jnp.bfloat16), own_sum[token_count:].astype(jnp.bfloat16))


def solution(mesh):
    nodes = mesh.shape["node"]
    locals_ = mesh.shape["local"]
    grid = jax.sharding.Mesh(mesh.devices.reshape(nodes, 2, locals_ // 2), ("node", "half", "sub"))
    rows = P(("node", "half", "sub"), None)
    stack = P(("node", "half", "sub"), None, None)
    return jax.shard_map(
        per_device,
        mesh=grid,
        in_specs=(rows, rows, rows, rows, stack, stack, stack),
        out_specs=(rows, rows),
        check_vma=False,
    )
```

```python
import jax
import jax.numpy as jnp
from jax import lax
from jax.sharding import PartitionSpec as P


def expert_rows(inputs, upstream, both_w, down_w):
    ff = down_w.shape[0]
    joint = jnp.dot(inputs, both_w, preferred_element_type=jnp.float32)
    gate = joint[:, :ff]
    lifted = joint[:, ff:]
    sigma = jax.nn.sigmoid(gate)
    active = (gate * sigma * lifted).astype(jnp.bfloat16)
    result = jnp.dot(active, down_w, preferred_element_type=jnp.float32).astype(jnp.bfloat16)
    contract = (((1,), (1,)), ((), ()))
    back = lax.dot_general(upstream, down_w, contract, preferred_element_type=jnp.float32)
    d_gate = (back * lifted * sigma * (1.0 + gate * (1.0 - sigma))).astype(jnp.bfloat16)
    d_lift = (back * gate * sigma).astype(jnp.bfloat16)
    grads = lax.dot_general(jnp.concatenate([d_gate, d_lift], axis=1), both_w, contract, preferred_element_type=jnp.float32)
    return result, grads.astype(jnp.bfloat16)


def row_slots(expert_ids, experts, capacity):
    flat_ids = expert_ids.reshape(-1)
    onehot = (flat_ids[:, None] == jnp.arange(experts, dtype=jnp.int32)[None, :]).astype(jnp.int32)
    ranks = jnp.sum((jnp.cumsum(onehot, axis=0) - 1) * onehot, axis=1)
    return flat_ids * capacity + ranks


def inward(buffer):
    return lax.all_to_all(buffer, ("node", "sub"), split_axis=0, concat_axis=0, tiled=True)


def split_three(weights):
    high = lax.reduce_precision(weights, exponent_bits=8, mantissa_bits=7)
    rest = weights - high
    middle = lax.reduce_precision(rest, exponent_bits=8, mantissa_bits=7)
    low = rest - middle
    return [part.astype(jnp.bfloat16) for part in (high, middle, low)]


def chunk_rows(group_size, slots_per):
    main = slots_per // 8 * 8
    tail = slots_per - main
    place = jnp.arange(2 * slots_per, dtype=jnp.int32)
    in_tail = place >= 2 * main
    rank = jnp.where(in_tail, main + (place - 2 * main) % max(tail, 1), place % max(main, 1))
    part = jnp.where(in_tail, (place - 2 * main) // max(tail, 1), place // max(main, 1))
    row_slot = (jnp.arange(group_size, dtype=jnp.int32)[:, None] * slots_per + rank[None, :]).reshape(-1)
    return row_slot, jnp.tile(part, group_size) == 0


def route(ids, near, group, group_size, slots_per):
    flat = jnp.where(near, group, group_size).reshape(-1)
    onehot = (flat[:, None] == jnp.arange(group_size, dtype=jnp.int32)[None, :]).astype(jnp.int32)
    ranks = jnp.sum((jnp.cumsum(onehot, axis=0) - 1) * onehot, axis=1)
    return jnp.where(flat < group_size, flat * slots_per + ranks, -1).reshape(ids.shape)


def pack(slots, inputs, upstream, row_slot, first):
    hits = slots[None, :, :] == row_slot[:, None, None]
    taken = jnp.any(hits, axis=2).astype(jnp.bfloat16)
    blank = jnp.zeros_like(taken)
    dispatch = jnp.concatenate([jnp.where(first[:, None], taken, blank), jnp.where(first[:, None], blank, taken)], axis=1)
    source = jnp.concatenate([inputs, upstream], axis=0)
    return jnp.dot(dispatch, source, preferred_element_type=jnp.float32).astype(jnp.bfloat16)


def combine(slots, wts, returned, row_slot, first):
    spread = jnp.where(slots[None, :, :] == row_slot[:, None, None], wts[None, :, :], 0.0).sum(axis=2).T
    zero = jnp.zeros_like(spread)
    weights = jnp.concatenate([jnp.where(first[None, :], spread, zero), jnp.where(first[None, :], zero, spread)], axis=0)
    parts = jnp.concatenate(split_three(weights), axis=0)
    summed = jnp.dot(parts, returned, preferred_element_type=jnp.float32)
    return summed.reshape(3, weights.shape[0], returned.shape[1]).sum(axis=0)


def unpack(received, main, tail):
    group_size, _, width = received.shape
    inputs = [received[:, :main].reshape(group_size * main, width)]
    upstream = [received[:, main:2 * main].reshape(group_size * main, width)]
    if tail:
        ends = received[:, 2 * main:].reshape(group_size, 2, tail, width)
        inputs.append(ends[:, 0].reshape(group_size * tail, width))
        upstream.append(ends[:, 1].reshape(group_size * tail, width))
    return inputs, upstream


def repack(result, grads, group_size, main, tail):
    width = result.shape[1]
    edge = group_size * main
    pieces = [result[:edge].reshape(group_size, main, width), grads[:edge].reshape(group_size, main, width)]
    if tail:
        pieces += [result[edge:].reshape(group_size, tail, width), grads[edge:].reshape(group_size, tail, width)]
    return jnp.concatenate(pieces, axis=1)


def per_device(tokens, grad_out, expert_ids, combine_w, w_gate, w_up, w_down):
    token_count, width = tokens.shape
    top_count = expert_ids.shape[1]
    halves = lax.axis_size("half")
    subs = lax.axis_size("sub")
    group_size = lax.axis_size("node") * subs
    experts = group_size * halves
    capacity = max(2, (5 * token_count * top_count + 4 * experts - 1) // (4 * experts))
    slots_per = (capacity + 3) // 4 * 4
    main = slots_per // 8 * 8
    tail = slots_per - main
    row_slot, first = chunk_rows(group_size, slots_per)
    swap = [(i, (i + 1) % halves) for i in range(halves)]
    here = lax.axis_index("half")
    far_stacked = lax.ppermute(jnp.concatenate([tokens, grad_out], axis=0), "half", swap)
    far_ids = lax.ppermute(expert_ids, "half", swap)
    far_w = lax.ppermute(combine_w, "half", swap)

    def near_slots(ids):
        near = (ids % (halves * subs)) // subs == here
        group = (ids // (halves * subs)) * subs + ids % subs
        return route(ids, near, group, group_size, slots_per)

    both_w = jnp.concatenate([w_gate[0], w_up[0]], axis=1)
    own_slots = near_slots(expert_ids)
    far_slots = near_slots(far_ids)
    own_sent = inward(pack(own_slots, tokens, grad_out, row_slot, first).reshape(group_size, 2 * slots_per, width))
    own_in, own_up = unpack(own_sent, main, tail)
    own_res, own_grads = expert_rows(jnp.concatenate(own_in, axis=0), jnp.concatenate(own_up, axis=0),
                                     both_w, w_down[0])
    own_packed = repack(own_res, own_grads, group_size, main, tail)
    far_stacked, far_w, own_sent = lax.optimization_barrier((far_stacked, far_w, own_sent))
    far_slots = near_slots(far_ids)
    far_sent = pack(far_slots, far_stacked[:token_count], far_stacked[token_count:], row_slot, first)
    far_sent = inward(far_sent.reshape(group_size, 2 * slots_per, width))
    far_sent, own_packed = lax.optimization_barrier((far_sent, own_packed))
    own_back = inward(own_packed)
    half_rows = group_size * slots_per
    own_sum = combine(own_slots, combine_w, own_back.reshape(2 * half_rows, width), row_slot, first)
    far_in, far_up = unpack(far_sent, main, tail)
    far_res, far_grads = expert_rows(jnp.concatenate(far_in, axis=0), jnp.concatenate(far_up, axis=0),
                                     both_w, w_down[0])
    far_packed, own_back = lax.optimization_barrier((repack(far_res, far_grads, group_size, main, tail), own_back))
    far_back = inward(far_packed)
    far_sum = combine(far_slots, far_w, far_back.reshape(2 * half_rows, width), row_slot, first).astype(jnp.bfloat16)
    near_part = lax.ppermute(far_sum, "half", swap).astype(jnp.float32)
    own_sum = own_sum + near_part
    return (own_sum[:token_count].astype(jnp.bfloat16), own_sum[token_count:].astype(jnp.bfloat16))


def solution(mesh):
    nodes = mesh.shape["node"]
    locals_ = mesh.shape["local"]
    grid = jax.sharding.Mesh(mesh.devices.reshape(nodes, 2, locals_ // 2), ("node", "half", "sub"))
    rows = P(("node", "half", "sub"), None)
    stack = P(("node", "half", "sub"), None, None)
    return jax.shard_map(
        per_device,
        mesh=grid,
        in_specs=(rows, rows, rows, rows, stack, stack, stack),
        out_specs=(rows, rows),
        check_vma=False,
    )
```

```python
import jax
import jax.numpy as jnp
from jax import lax
from jax.sharding import PartitionSpec as P


def expert_rows(inputs, upstream, both_w, down_w):
    ff = down_w.shape[0]
    joint = jnp.dot(inputs, both_w, preferred_element_type=jnp.float32)
    gate = joint[:, :ff]
    lifted = joint[:, ff:]
    sigma = jax.nn.sigmoid(gate)
    active = (gate * sigma * lifted).astype(jnp.bfloat16)
    result = jnp.dot(active, down_w, preferred_element_type=jnp.float32).astype(jnp.bfloat16)
    contract = (((1,), (1,)), ((), ()))
    back = lax.dot_general(upstream, down_w, contract, preferred_element_type=jnp.float32)
    d_gate = (back * lifted * sigma * (1.0 + gate * (1.0 - sigma))).astype(jnp.bfloat16)
    d_lift = (back * gate * sigma).astype(jnp.bfloat16)
    grads = lax.dot_general(jnp.concatenate([d_gate, d_lift], axis=1), both_w, contract, preferred_element_type=jnp.float32)
    return result, grads.astype(jnp.bfloat16)


def row_slots(expert_ids, experts, capacity):
    flat_ids = expert_ids.reshape(-1)
    onehot = (flat_ids[:, None] == jnp.arange(experts, dtype=jnp.int32)[None, :]).astype(jnp.int32)
    ranks = jnp.sum((jnp.cumsum(onehot, axis=0) - 1) * onehot, axis=1)
    return flat_ids * capacity + ranks


def inward(buffer):
    return lax.all_to_all(buffer, ("node", "sub"), split_axis=0, concat_axis=0, tiled=True)


def split_weights(weights):
    high = lax.reduce_precision(weights, exponent_bits=8, mantissa_bits=7)
    middle = weights - high
    return [part.astype(jnp.bfloat16) for part in (high, middle)]


def chunk_rows(group_size, slots_per):
    main = slots_per // 8 * 8
    tail = slots_per - main
    place = jnp.arange(2 * slots_per, dtype=jnp.int32)
    in_tail = place >= 2 * main
    rank = jnp.where(in_tail, main + (place - 2 * main) % max(tail, 1), place % max(main, 1))
    part = jnp.where(in_tail, (place - 2 * main) // max(tail, 1), place // max(main, 1))
    row_slot = (jnp.arange(group_size, dtype=jnp.int32)[:, None] * slots_per + rank[None, :]).reshape(-1)
    return row_slot, jnp.tile(part, group_size) == 0


def route(ids, near, group, group_size, slots_per):
    flat = jnp.where(near, group, group_size).reshape(-1)
    onehot = (flat[:, None] == jnp.arange(group_size, dtype=jnp.int32)[None, :]).astype(jnp.int32)
    ranks = jnp.sum((jnp.cumsum(onehot, axis=0) - 1) * onehot, axis=1)
    return jnp.where(flat < group_size, flat * slots_per + ranks, -1).reshape(ids.shape)


def pack(slots, inputs, upstream, row_slot, first):
    hits = slots[None, :, :] == row_slot[:, None, None]
    taken = jnp.any(hits, axis=2).astype(jnp.bfloat16)
    blank = jnp.zeros_like(taken)
    dispatch = jnp.concatenate([jnp.where(first[:, None], taken, blank), jnp.where(first[:, None], blank, taken)], axis=1)
    source = jnp.concatenate([inputs, upstream], axis=0)
    return jnp.dot(dispatch, source, preferred_element_type=jnp.float32).astype(jnp.bfloat16)


def combine(slots, wts, returned, row_slot, first):
    spread = jnp.where(slots[None, :, :] == row_slot[:, None, None], wts[None, :, :], 0.0).sum(axis=2).T
    zero = jnp.zeros_like(spread)
    weights = jnp.concatenate([jnp.where(first[None, :], spread, zero), jnp.where(first[None, :], zero, spread)], axis=0)
    parts = jnp.concatenate(split_weights(weights), axis=0)
    summed = jnp.dot(parts, returned, preferred_element_type=jnp.float32)
    return summed.reshape(2, weights.shape[0], returned.shape[1]).sum(axis=0)


def unpack(received, main, tail):
    group_size, _, width = received.shape
    inputs = [received[:, :main].reshape(group_size * main, width)]
    upstream = [received[:, main:2 * main].reshape(group_size * main, width)]
    if tail:
        ends = received[:, 2 * main:].reshape(group_size, 2, tail, width)
        inputs.append(ends[:, 0].reshape(group_size * tail, width))
        upstream.append(ends[:, 1].reshape(group_size * tail, width))
    return inputs, upstream


def repack(result, grads, group_size, main, tail):
    width = result.shape[1]
    edge = group_size * main
    pieces = [result[:edge].reshape(group_size, main, width), grads[:edge].reshape(group_size, main, width)]
    if tail:
        pieces += [result[edge:].reshape(group_size, tail, width), grads[edge:].reshape(group_size, tail, width)]
    return jnp.concatenate(pieces, axis=1)


def per_device(tokens, grad_out, expert_ids, combine_w, w_gate, w_up, w_down):
    token_count, width = tokens.shape
    top_count = expert_ids.shape[1]
    halves = lax.axis_size("half")
    subs = lax.axis_size("sub")
    group_size = lax.axis_size("node") * subs
    experts = group_size * halves
    capacity = max(2, (5 * token_count * top_count + 4 * experts - 1) // (4 * experts))
    slots_per = (capacity + 3) // 4 * 4
    main = slots_per // 8 * 8
    tail = slots_per - main
    row_slot, first = chunk_rows(group_size, slots_per)
    swap = [(i, (i + 1) % halves) for i in range(halves)]
    here = lax.axis_index("half")
    far_stacked = lax.ppermute(jnp.concatenate([tokens, grad_out], axis=0), "half", swap)
    far_ids = lax.ppermute(expert_ids, "half", swap)
    far_w = lax.ppermute(combine_w, "half", swap)

    def near_slots(ids):
        near = (ids % (halves * subs)) // subs == here
        group = (ids // (halves * subs)) * subs + ids % subs
        return route(ids, near, group, group_size, slots_per)

    both_w = jnp.concatenate([w_gate[0], w_up[0]], axis=1)
    own_slots = near_slots(expert_ids)
    far_slots = near_slots(far_ids)
    own_sent = inward(pack(own_slots, tokens, grad_out, row_slot, first).reshape(group_size, 2 * slots_per, width))
    far_stacked, far_w, own_sent = lax.optimization_barrier((far_stacked, far_w, own_sent))
    far_sent = pack(far_slots, far_stacked[:token_count], far_stacked[token_count:], row_slot, first)
    far_sent = inward(far_sent.reshape(group_size, 2 * slots_per, width))
    own_in, own_up = unpack(own_sent, main, tail)
    own_res, own_grads = expert_rows(jnp.concatenate(own_in, axis=0), jnp.concatenate(own_up, axis=0),
                                     both_w, w_down[0])
    own_packed = repack(own_res, own_grads, group_size, main, tail)
    far_in, far_up = unpack(far_sent, main, tail)
    far_res, far_grads = expert_rows(jnp.concatenate(far_in, axis=0), jnp.concatenate(far_up, axis=0),
                                     both_w, w_down[0])
    half_rows = group_size * slots_per
    far_back = inward(repack(far_res, far_grads, group_size, main, tail))
    far_back, own_packed = lax.optimization_barrier((far_back, own_packed))
    far_sum = combine(far_slots, far_w, far_back.reshape(2 * half_rows, width), row_slot, first).astype(jnp.bfloat16)
    near_part = lax.ppermute(far_sum, "half", swap).astype(jnp.float32)
    own_back = inward(own_packed)
    own_sum = combine(own_slots, combine_w, own_back.reshape(2 * half_rows, width), row_slot, first) + near_part
    return (own_sum[:token_count].astype(jnp.bfloat16), own_sum[token_count:].astype(jnp.bfloat16))


def solution(mesh):
    nodes = mesh.shape["node"]
    locals_ = mesh.shape["local"]
    grid = jax.sharding.Mesh(mesh.devices.reshape(nodes, 2, locals_ // 2), ("node", "half", "sub"))
    rows = P(("node", "half", "sub"), None)
    stack = P(("node", "half", "sub"), None, None)
    return jax.shard_map(
        per_device,
        mesh=grid,
        in_specs=(rows, rows, rows, rows, stack, stack, stack),
        out_specs=(rows, rows),
        check_vma=False,
    )
```

```python
import jax
import jax.numpy as jnp
from jax import lax
from jax.sharding import PartitionSpec as P


def expert_rows(inputs, upstream, both_w, down_w):
    ff = down_w.shape[0]
    joint = jnp.dot(inputs, both_w, preferred_element_type=jnp.float32)
    gate = joint[:, :ff]
    lifted = joint[:, ff:]
    sigma = jax.nn.sigmoid(gate)
    active = (gate * sigma * lifted).astype(jnp.bfloat16)
    result = jnp.dot(active, down_w, preferred_element_type=jnp.float32).astype(jnp.bfloat16)
    contract = (((1,), (1,)), ((), ()))
    back = lax.dot_general(upstream, down_w, contract, preferred_element_type=jnp.float32)
    d_gate = (back * lifted * sigma * (1.0 + gate * (1.0 - sigma))).astype(jnp.bfloat16)
    d_lift = (back * gate * sigma).astype(jnp.bfloat16)
    grads = lax.dot_general(jnp.concatenate([d_gate, d_lift], axis=1), both_w, contract, preferred_element_type=jnp.float32)
    return result, grads.astype(jnp.bfloat16)


def row_slots(expert_ids, experts, capacity):
    flat_ids = expert_ids.reshape(-1)
    onehot = (flat_ids[:, None] == jnp.arange(experts, dtype=jnp.int32)[None, :]).astype(jnp.int32)
    ranks = jnp.sum((jnp.cumsum(onehot, axis=0) - 1) * onehot, axis=1)
    return flat_ids * capacity + ranks


def inward(buffer):
    return lax.all_to_all(buffer, ("node", "sub"), split_axis=0, concat_axis=0, tiled=True)


def split_weights(weights):
    high = lax.reduce_precision(weights, exponent_bits=8, mantissa_bits=7)
    middle = weights - high
    return [part.astype(jnp.bfloat16) for part in (high, middle)]


def chunk_rows(group_size, slots_per):
    main = slots_per // 8 * 8
    tail = slots_per - main
    place = jnp.arange(2 * slots_per, dtype=jnp.int32)
    in_tail = place >= 2 * main
    rank = jnp.where(in_tail, main + (place - 2 * main) % max(tail, 1), place % max(main, 1))
    part = jnp.where(in_tail, (place - 2 * main) // max(tail, 1), place // max(main, 1))
    row_slot = (jnp.arange(group_size, dtype=jnp.int32)[:, None] * slots_per + rank[None, :]).reshape(-1)
    return row_slot, jnp.tile(part, group_size) == 0


def route(ids, near, group, group_size, slots_per):
    flat = jnp.where(near, group, group_size).reshape(-1)
    onehot = (flat[:, None] == jnp.arange(group_size, dtype=jnp.int32)[None, :]).astype(jnp.int32)
    ranks = jnp.sum((jnp.cumsum(onehot, axis=0) - 1) * onehot, axis=1)
    return jnp.where(flat < group_size, flat * slots_per + ranks, -1).reshape(ids.shape)


def pack(slots, inputs, upstream, row_slot, first):
    hits = slots[None, :, :] == row_slot[:, None, None]
    taken = jnp.any(hits, axis=2).astype(jnp.bfloat16)
    blank = jnp.zeros_like(taken)
    dispatch = jnp.concatenate([jnp.where(first[:, None], taken, blank), jnp.where(first[:, None], blank, taken)], axis=1)
    source = jnp.concatenate([inputs, upstream], axis=0)
    return jnp.dot(dispatch, source, preferred_element_type=jnp.float32).astype(jnp.bfloat16)


def combine(slots, wts, returned, row_slot, first):
    spread = jnp.where(slots[None, :, :] == row_slot[:, None, None], wts[None, :, :], 0.0).sum(axis=2).T
    zero = jnp.zeros_like(spread)
    weights = jnp.concatenate([jnp.where(first[None, :], spread, zero), jnp.where(first[None, :], zero, spread)], axis=0)
    parts = jnp.concatenate(split_weights(weights), axis=0)
    summed = jnp.dot(parts, returned, preferred_element_type=jnp.float32)
    return summed.reshape(2, weights.shape[0], returned.shape[1]).sum(axis=0)


def unpack(received, main, tail):
    group_size, _, width = received.shape
    inputs = [received[:, :main].reshape(group_size * main, width)]
    upstream = [received[:, main:2 * main].reshape(group_size * main, width)]
    if tail:
        ends = received[:, 2 * main:].reshape(group_size, 2, tail, width)
        inputs.append(ends[:, 0].reshape(group_size * tail, width))
        upstream.append(ends[:, 1].reshape(group_size * tail, width))
    return inputs, upstream


def repack(result, grads, group_size, main, tail):
    width = result.shape[1]
    edge = group_size * main
    pieces = [result[:edge].reshape(group_size, main, width), grads[:edge].reshape(group_size, main, width)]
    if tail:
        pieces += [result[edge:].reshape(group_size, tail, width), grads[edge:].reshape(group_size, tail, width)]
    return jnp.concatenate(pieces, axis=1)


def per_device(tokens, grad_out, expert_ids, combine_w, w_gate, w_up, w_down):
    token_count, width = tokens.shape
    top_count = expert_ids.shape[1]
    halves = lax.axis_size("half")
    subs = lax.axis_size("sub")
    group_size = lax.axis_size("node") * subs
    experts = group_size * halves
    capacity = max(2, (5 * token_count * top_count + 4 * experts - 1) // (4 * experts))
    slots_per = (capacity + 3) // 4 * 4
    main = slots_per // 8 * 8
    tail = slots_per - main
    row_slot, first = chunk_rows(group_size, slots_per)
    swap = [(i, (i + 1) % halves) for i in range(halves)]
    here = lax.axis_index("half")
    far_stacked = lax.ppermute(jnp.concatenate([tokens, grad_out], axis=0), "half", swap)
    far_meta = lax.ppermute(jnp.concatenate([expert_ids.astype(jnp.float32), combine_w], axis=1), "half", swap)
    far_ids = far_meta[:, :top_count].astype(jnp.int32)
    far_w = far_meta[:, top_count:]

    def near_slots(ids):
        near = (ids % (halves * subs)) // subs == here
        group = (ids // (halves * subs)) * subs + ids % subs
        return route(ids, near, group, group_size, slots_per)

    both_w = jnp.concatenate([w_gate[0], w_up[0]], axis=1)
    own_slots = near_slots(expert_ids)
    far_slots = near_slots(far_ids)
    own_sent = inward(pack(own_slots, tokens, grad_out, row_slot, first).reshape(group_size, 2 * slots_per, width))
    far_stacked, far_w, own_sent = lax.optimization_barrier((far_stacked, far_w, own_sent))
    far_sent = pack(far_slots, far_stacked[:token_count], far_stacked[token_count:], row_slot, first)
    far_sent = inward(far_sent.reshape(group_size, 2 * slots_per, width))
    own_in, own_up = unpack(own_sent, main, tail)
    own_res, own_grads = expert_rows(jnp.concatenate(own_in, axis=0), jnp.concatenate(own_up, axis=0),
                                     both_w, w_down[0])
    own_packed = repack(own_res, own_grads, group_size, main, tail)
    far_in, far_up = unpack(far_sent, main, tail)
    far_res, far_grads = expert_rows(jnp.concatenate(far_in, axis=0), jnp.concatenate(far_up, axis=0),
                                     both_w, w_down[0])
    half_rows = group_size * slots_per
    far_back = inward(repack(far_res, far_grads, group_size, main, tail))
    far_back, own_packed = lax.optimization_barrier((far_back, own_packed))
    far_sum = combine(far_slots, far_w, far_back.reshape(2 * half_rows, width), row_slot, first).astype(jnp.bfloat16)
    near_part = lax.ppermute(far_sum, "half", swap).astype(jnp.float32)
    own_back = inward(own_packed)
    own_sum = combine(own_slots, combine_w, own_back.reshape(2 * half_rows, width), row_slot, first) + near_part
    return (own_sum[:token_count].astype(jnp.bfloat16), own_sum[token_count:].astype(jnp.bfloat16))


def solution(mesh):
    nodes = mesh.shape["node"]
    locals_ = mesh.shape["local"]
    grid = jax.sharding.Mesh(mesh.devices.reshape(nodes, 2, locals_ // 2), ("node", "half", "sub"))
    rows = P(("node", "half", "sub"), None)
    stack = P(("node", "half", "sub"), None, None)
    return jax.shard_map(
        per_device,
        mesh=grid,
        in_specs=(rows, rows, rows, rows, stack, stack, stack),
        out_specs=(rows, rows),
        check_vma=False,
    )
```

```python
import jax
import jax.numpy as jnp
from jax import lax
from jax.sharding import PartitionSpec as P


def expert_rows(inputs, upstream, both_w, down_w):
    ff = down_w.shape[0]
    joint = jnp.dot(inputs, both_w, preferred_element_type=jnp.float32)
    gate = joint[:, :ff]
    lifted = joint[:, ff:]
    sigma = jax.nn.sigmoid(gate)
    active = (gate * sigma * lifted).astype(jnp.bfloat16)
    result = jnp.dot(active, down_w, preferred_element_type=jnp.float32).astype(jnp.bfloat16)
    contract = (((1,), (1,)), ((), ()))
    back = lax.dot_general(upstream, down_w, contract, preferred_element_type=jnp.float32)
    d_gate = (back * lifted * sigma * (1.0 + gate * (1.0 - sigma))).astype(jnp.bfloat16)
    d_lift = (back * gate * sigma).astype(jnp.bfloat16)
    grads = lax.dot_general(jnp.concatenate([d_gate, d_lift], axis=1), both_w, contract, preferred_element_type=jnp.float32)
    return result, grads.astype(jnp.bfloat16)


def row_slots(expert_ids, experts, capacity):
    flat_ids = expert_ids.reshape(-1)
    onehot = (flat_ids[:, None] == jnp.arange(experts, dtype=jnp.int32)[None, :]).astype(jnp.int32)
    ranks = jnp.sum((jnp.cumsum(onehot, axis=0) - 1) * onehot, axis=1)
    return flat_ids * capacity + ranks


def inward(buffer):
    return lax.all_to_all(buffer, ("node", "sub"), split_axis=0, concat_axis=0, tiled=True)


def split_weights(weights):
    high = lax.reduce_precision(weights, exponent_bits=8, mantissa_bits=7)
    middle = weights - high
    return [part.astype(jnp.bfloat16) for part in (high, middle)]


def chunk_rows(group_size, slots_per):
    main = slots_per // 8 * 8
    tail = slots_per - main
    place = jnp.arange(2 * slots_per, dtype=jnp.int32)
    in_tail = place >= 2 * main
    rank = jnp.where(in_tail, main + (place - 2 * main) % max(tail, 1), place % max(main, 1))
    part = jnp.where(in_tail, (place - 2 * main) // max(tail, 1), place // max(main, 1))
    row_slot = (jnp.arange(group_size, dtype=jnp.int32)[:, None] * slots_per + rank[None, :]).reshape(-1)
    return row_slot, jnp.tile(part, group_size) == 0


def route(ids, near, group, group_size, slots_per):
    flat = jnp.where(near, group, group_size).reshape(-1)
    onehot = (flat[:, None] == jnp.arange(group_size, dtype=jnp.int32)[None, :]).astype(jnp.int32)
    ranks = jnp.sum((jnp.cumsum(onehot, axis=0) - 1) * onehot, axis=1)
    return jnp.where(flat < group_size, flat * slots_per + ranks, -1).reshape(ids.shape)


def pack(slots, inputs, upstream, row_slot, first):
    hits = slots[None, :, :] == row_slot[:, None, None]
    taken = jnp.any(hits, axis=2).astype(jnp.bfloat16)
    blank = jnp.zeros_like(taken)
    dispatch = jnp.concatenate([jnp.where(first[:, None], taken, blank), jnp.where(first[:, None], blank, taken)], axis=1)
    source = jnp.concatenate([inputs, upstream], axis=0)
    return jnp.dot(dispatch, source, preferred_element_type=jnp.float32).astype(jnp.bfloat16)


def combine(slots, wts, returned, row_slot, first):
    spread = jnp.where(slots[None, :, :] == row_slot[:, None, None], wts[None, :, :], 0.0).sum(axis=2).T
    zero = jnp.zeros_like(spread)
    weights = jnp.concatenate([jnp.where(first[None, :], spread, zero), jnp.where(first[None, :], zero, spread)], axis=0)
    parts = jnp.concatenate(split_weights(weights), axis=0)
    summed = jnp.dot(parts, returned, preferred_element_type=jnp.float32)
    return summed.reshape(2, weights.shape[0], returned.shape[1]).sum(axis=0)


def unpack(received, main, tail):
    group_size, _, width = received.shape
    inputs = [received[:, :main].reshape(group_size * main, width)]
    upstream = [received[:, main:2 * main].reshape(group_size * main, width)]
    if tail:
        ends = received[:, 2 * main:].reshape(group_size, 2, tail, width)
        inputs.append(ends[:, 0].reshape(group_size * tail, width))
        upstream.append(ends[:, 1].reshape(group_size * tail, width))
    return inputs, upstream


def repack(result, grads, group_size, main, tail):
    width = result.shape[1]
    edge = group_size * main
    pieces = [result[:edge].reshape(group_size, main, width), grads[:edge].reshape(group_size, main, width)]
    if tail:
        pieces += [result[edge:].reshape(group_size, tail, width), grads[edge:].reshape(group_size, tail, width)]
    return jnp.concatenate(pieces, axis=1)


def per_device(tokens, grad_out, expert_ids, combine_w, w_gate, w_up, w_down):
    token_count, width = tokens.shape
    top_count = expert_ids.shape[1]
    halves = lax.axis_size("half")
    subs = lax.axis_size("sub")
    group_size = lax.axis_size("node") * subs
    experts = group_size * halves
    capacity = max(2, (5 * token_count * top_count + 4 * experts - 1) // (4 * experts))
    slots_per = (capacity + 3) // 4 * 4
    main = slots_per // 8 * 8
    tail = slots_per - main
    row_slot, first = chunk_rows(group_size, slots_per)
    swap = [(i, (i + 1) % halves) for i in range(halves)]
    here = lax.axis_index("half")
    far_stacked = lax.ppermute(jnp.concatenate([tokens, grad_out], axis=0), "half", swap)

    def near_slots(ids):
        near = (ids % (halves * subs)) // subs == here
        group = (ids // (halves * subs)) * subs + ids % subs
        return route(ids, near, group, group_size, slots_per)

    both_w = jnp.concatenate([w_gate[0], w_up[0]], axis=1)
    own_slots = near_slots(expert_ids)
    own_buffer = pack(own_slots, tokens, grad_out, row_slot, first)
    sent_ids, sent_w, own_buffer = lax.optimization_barrier((expert_ids, combine_w, own_buffer))
    far_ids = lax.ppermute(sent_ids, "half", swap)
    far_w = lax.ppermute(sent_w, "half", swap)
    far_slots = near_slots(far_ids)
    own_sent = inward(own_buffer.reshape(group_size, 2 * slots_per, width))
    far_stacked, far_w, own_sent = lax.optimization_barrier((far_stacked, far_w, own_sent))
    far_sent = pack(far_slots, far_stacked[:token_count], far_stacked[token_count:], row_slot, first)
    far_sent = inward(far_sent.reshape(group_size, 2 * slots_per, width))
    own_in, own_up = unpack(own_sent, main, tail)
    own_res, own_grads = expert_rows(jnp.concatenate(own_in, axis=0), jnp.concatenate(own_up, axis=0),
                                     both_w, w_down[0])
    own_packed = repack(own_res, own_grads, group_size, main, tail)
    far_in, far_up = unpack(far_sent, main, tail)
    far_res, far_grads = expert_rows(jnp.concatenate(far_in, axis=0), jnp.concatenate(far_up, axis=0),
                                     both_w, w_down[0])
    half_rows = group_size * slots_per
    far_back = inward(repack(far_res, far_grads, group_size, main, tail))
    far_back, own_packed = lax.optimization_barrier((far_back, own_packed))
    far_sum = combine(far_slots, far_w, far_back.reshape(2 * half_rows, width), row_slot, first).astype(jnp.bfloat16)
    near_part = lax.ppermute(far_sum, "half", swap).astype(jnp.float32)
    own_back = inward(own_packed)
    own_sum = combine(own_slots, combine_w, own_back.reshape(2 * half_rows, width), row_slot, first) + near_part
    return (own_sum[:token_count].astype(jnp.bfloat16), own_sum[token_count:].astype(jnp.bfloat16))


def solution(mesh):
    nodes = mesh.shape["node"]
    locals_ = mesh.shape["local"]
    grid = jax.sharding.Mesh(mesh.devices.reshape(nodes, 2, locals_ // 2), ("node", "half", "sub"))
    rows = P(("node", "half", "sub"), None)
    stack = P(("node", "half", "sub"), None, None)
    return jax.shard_map(
        per_device,
        mesh=grid,
        in_specs=(rows, rows, rows, rows, stack, stack, stack),
        out_specs=(rows, rows),
        check_vma=False,
    )
```

```python
import jax
import jax.numpy as jnp
from jax import lax
from jax.sharding import PartitionSpec as P


def expert_rows(inputs, upstream, both_w, down_w):
    ff = down_w.shape[0]
    joint = jnp.dot(inputs, both_w, preferred_element_type=jnp.float32)
    gate = joint[:, :ff]
    lifted = joint[:, ff:]
    sigma = jax.nn.sigmoid(gate)
    active = (gate * sigma * lifted).astype(jnp.bfloat16)
    result = jnp.dot(active, down_w, preferred_element_type=jnp.float32).astype(jnp.bfloat16)
    contract = (((1,), (1,)), ((), ()))
    back = lax.dot_general(upstream, down_w, contract, preferred_element_type=jnp.float32)
    d_gate = (back * lifted * sigma * (1.0 + gate * (1.0 - sigma))).astype(jnp.bfloat16)
    d_lift = (back * gate * sigma).astype(jnp.bfloat16)
    grads = lax.dot_general(jnp.concatenate([d_gate, d_lift], axis=1), both_w, contract, preferred_element_type=jnp.float32)
    return result, grads.astype(jnp.bfloat16)


def row_slots(expert_ids, experts, capacity):
    flat_ids = expert_ids.reshape(-1)
    onehot = (flat_ids[:, None] == jnp.arange(experts, dtype=jnp.int32)[None, :]).astype(jnp.int32)
    ranks = jnp.sum((jnp.cumsum(onehot, axis=0) - 1) * onehot, axis=1)
    return flat_ids * capacity + ranks


def inward(buffer):
    return lax.all_to_all(buffer, ("node", "sub"), split_axis=0, concat_axis=0, tiled=True)


def split_weights(weights):
    high = lax.reduce_precision(weights, exponent_bits=8, mantissa_bits=7)
    middle = weights - high
    return [part.astype(jnp.bfloat16) for part in (high, middle)]


def chunk_rows(group_size, slots_per):
    main = slots_per // 8 * 8
    tail = slots_per - main
    place = jnp.arange(2 * slots_per, dtype=jnp.int32)
    in_tail = place >= 2 * main
    rank = jnp.where(in_tail, main + (place - 2 * main) % max(tail, 1), place % max(main, 1))
    part = jnp.where(in_tail, (place - 2 * main) // max(tail, 1), place // max(main, 1))
    row_slot = (jnp.arange(group_size, dtype=jnp.int32)[:, None] * slots_per + rank[None, :]).reshape(-1)
    return row_slot, jnp.tile(part, group_size) == 0


def route(ids, near, group, group_size, slots_per):
    flat = jnp.where(near, group, group_size).reshape(-1)
    onehot = (flat[:, None] == jnp.arange(group_size, dtype=jnp.int32)[None, :]).astype(jnp.int32)
    ranks = jnp.sum((jnp.cumsum(onehot, axis=0) - 1) * onehot, axis=1)
    return jnp.where(flat < group_size, flat * slots_per + ranks, -1).reshape(ids.shape)


def pack(slots, inputs, upstream, row_slot, first):
    hits = slots[None, :, :] == row_slot[:, None, None]
    taken = jnp.any(hits, axis=2).astype(jnp.bfloat16)
    blank = jnp.zeros_like(taken)
    dispatch = jnp.concatenate([jnp.where(first[:, None], taken, blank), jnp.where(first[:, None], blank, taken)], axis=1)
    source = jnp.concatenate([inputs, upstream], axis=0)
    return jnp.dot(dispatch, source, preferred_element_type=jnp.float32).astype(jnp.bfloat16)


def combine(slots, wts, returned, row_slot, first):
    spread = jnp.where(slots[None, :, :] == row_slot[:, None, None], wts[None, :, :], 0.0).sum(axis=2).T
    zero = jnp.zeros_like(spread)
    weights = jnp.concatenate([jnp.where(first[None, :], spread, zero), jnp.where(first[None, :], zero, spread)], axis=0)
    parts = jnp.concatenate(split_weights(weights), axis=0)
    summed = jnp.dot(parts, returned, preferred_element_type=jnp.float32)
    return summed.reshape(2, weights.shape[0], returned.shape[1]).sum(axis=0)


def combine_half(slots, wts, returned, row_slot, side):
    spread = jnp.where(slots[None, :, :] == row_slot[:, None, None], wts[None, :, :], 0.0).sum(axis=2).T
    weights = jnp.where(side[None, :], spread, jnp.zeros_like(spread))
    parts = jnp.concatenate(split_weights(weights), axis=0)
    summed = jnp.dot(parts, returned, preferred_element_type=jnp.float32)
    return summed.reshape(2, weights.shape[0], returned.shape[1]).sum(axis=0)


def unpack(received, main, tail):
    group_size, _, width = received.shape
    inputs = [received[:, :main].reshape(group_size * main, width)]
    upstream = [received[:, main:2 * main].reshape(group_size * main, width)]
    if tail:
        ends = received[:, 2 * main:].reshape(group_size, 2, tail, width)
        inputs.append(ends[:, 0].reshape(group_size * tail, width))
        upstream.append(ends[:, 1].reshape(group_size * tail, width))
    return inputs, upstream


def repack(result, grads, group_size, main, tail):
    width = result.shape[1]
    edge = group_size * main
    pieces = [result[:edge].reshape(group_size, main, width), grads[:edge].reshape(group_size, main, width)]
    if tail:
        pieces += [result[edge:].reshape(group_size, tail, width), grads[edge:].reshape(group_size, tail, width)]
    return jnp.concatenate(pieces, axis=1)


def per_device(tokens, grad_out, expert_ids, combine_w, w_gate, w_up, w_down):
    token_count, width = tokens.shape
    top_count = expert_ids.shape[1]
    halves = lax.axis_size("half")
    subs = lax.axis_size("sub")
    group_size = lax.axis_size("node") * subs
    experts = group_size * halves
    capacity = max(2, (5 * token_count * top_count + 4 * experts - 1) // (4 * experts))
    slots_per = (capacity + 3) // 4 * 4
    main = slots_per // 8 * 8
    tail = slots_per - main
    row_slot, first = chunk_rows(group_size, slots_per)
    swap = [(i, (i + 1) % halves) for i in range(halves)]
    here = lax.axis_index("half")
    far_stacked = lax.ppermute(jnp.concatenate([tokens, grad_out], axis=0), "half", swap)
    far_ids = lax.ppermute(expert_ids, "half", swap)
    far_w = lax.ppermute(combine_w, "half", swap)

    def near_slots(ids):
        near = (ids % (halves * subs)) // subs == here
        group = (ids // (halves * subs)) * subs + ids % subs
        return route(ids, near, group, group_size, slots_per)

    both_w = jnp.concatenate([w_gate[0], w_up[0]], axis=1)
    own_slots = near_slots(expert_ids)
    far_slots = near_slots(far_ids)
    own_sent = inward(pack(own_slots, tokens, grad_out, row_slot, first).reshape(group_size, 2 * slots_per, width))
    far_stacked, far_w, own_sent = lax.optimization_barrier((far_stacked, far_w, own_sent))
    far_sent = pack(far_slots, far_stacked[:token_count], far_stacked[token_count:], row_slot, first)
    far_sent = inward(far_sent.reshape(group_size, 2 * slots_per, width))
    own_in, own_up = unpack(own_sent, main, tail)
    own_res, own_grads = expert_rows(jnp.concatenate(own_in, axis=0), jnp.concatenate(own_up, axis=0),
                                     both_w, w_down[0])
    own_packed = repack(own_res, own_grads, group_size, main, tail)
    far_in, far_up = unpack(far_sent, main, tail)
    far_res, far_grads = expert_rows(jnp.concatenate(far_in, axis=0), jnp.concatenate(far_up, axis=0),
                                     both_w, w_down[0])
    half_rows = group_size * slots_per
    far_back = inward(repack(far_res, far_grads, group_size, main, tail))
    far_back, own_packed = lax.optimization_barrier((far_back, own_packed))
    far_rows = far_back.reshape(2 * half_rows, width)
    near_part = jnp.concatenate([
        lax.ppermute(combine_half(far_slots, far_w, far_rows, row_slot, side).astype(jnp.bfloat16), "half", swap)
        for side in (first, ~first)], axis=0).astype(jnp.float32)
    own_back = inward(own_packed)
    own_sum = combine(own_slots, combine_w, own_back.reshape(2 * half_rows, width), row_slot, first) + near_part
    return (own_sum[:token_count].astype(jnp.bfloat16), own_sum[token_count:].astype(jnp.bfloat16))


def solution(mesh):
    nodes = mesh.shape["node"]
    locals_ = mesh.shape["local"]
    grid = jax.sharding.Mesh(mesh.devices.reshape(nodes, 2, locals_ // 2), ("node", "half", "sub"))
    rows = P(("node", "half", "sub"), None)
    stack = P(("node", "half", "sub"), None, None)
    return jax.shard_map(
        per_device,
        mesh=grid,
        in_specs=(rows, rows, rows, rows, stack, stack, stack),
        out_specs=(rows, rows),
        check_vma=False,
    )
```

```python
import jax
import jax.numpy as jnp
from jax import lax
from jax.sharding import PartitionSpec as P


def expert_rows(inputs, upstream, both_w, down_w):
    ff = down_w.shape[0]
    joint = jnp.dot(inputs, both_w, preferred_element_type=jnp.float32)
    gate = joint[:, :ff]
    lifted = joint[:, ff:]
    sigma = jax.nn.sigmoid(gate)
    active = (gate * sigma * lifted).astype(jnp.bfloat16)
    result = jnp.dot(active, down_w, preferred_element_type=jnp.float32).astype(jnp.bfloat16)
    contract = (((1,), (1,)), ((), ()))
    back = lax.dot_general(upstream, down_w, contract, preferred_element_type=jnp.float32)
    d_gate = (back * lifted * sigma * (1.0 + gate * (1.0 - sigma))).astype(jnp.bfloat16)
    d_lift = (back * gate * sigma).astype(jnp.bfloat16)
    grads = lax.dot_general(jnp.concatenate([d_gate, d_lift], axis=1), both_w, contract, preferred_element_type=jnp.float32)
    return result, grads.astype(jnp.bfloat16)


def row_slots(expert_ids, experts, capacity):
    flat_ids = expert_ids.reshape(-1)
    onehot = (flat_ids[:, None] == jnp.arange(experts, dtype=jnp.int32)[None, :]).astype(jnp.int32)
    ranks = jnp.sum((jnp.cumsum(onehot, axis=0) - 1) * onehot, axis=1)
    return flat_ids * capacity + ranks


def inward(buffer):
    return lax.all_to_all(buffer, ("node", "sub"), split_axis=0, concat_axis=0, tiled=True)


def split_weights(weights):
    high = lax.reduce_precision(weights, exponent_bits=8, mantissa_bits=7)
    middle = weights - high
    return [part.astype(jnp.bfloat16) for part in (high, middle)]


def chunk_rows(group_size, slots_per):
    main = slots_per // 8 * 8
    tail = slots_per - main
    place = jnp.arange(2 * slots_per, dtype=jnp.int32)
    in_tail = place >= 2 * main
    rank = jnp.where(in_tail, main + (place - 2 * main) % max(tail, 1), place % max(main, 1))
    part = jnp.where(in_tail, (place - 2 * main) // max(tail, 1), place // max(main, 1))
    row_slot = (jnp.arange(group_size, dtype=jnp.int32)[:, None] * slots_per + rank[None, :]).reshape(-1)
    return row_slot, jnp.tile(part, group_size) == 0


def route(ids, near, group, group_size, slots_per):
    flat = jnp.where(near, group, group_size).reshape(-1)
    onehot = (flat[:, None] == jnp.arange(group_size, dtype=jnp.int32)[None, :]).astype(jnp.int32)
    ranks = jnp.sum((jnp.cumsum(onehot, axis=0) - 1) * onehot, axis=1)
    return jnp.where(flat < group_size, flat * slots_per + ranks, -1).reshape(ids.shape)


def pack(slots, inputs, upstream, row_slot, first):
    hits = slots[None, :, :] == row_slot[:, None, None]
    taken = jnp.any(hits, axis=2).astype(jnp.bfloat16)
    blank = jnp.zeros_like(taken)
    dispatch = jnp.concatenate([jnp.where(first[:, None], taken, blank), jnp.where(first[:, None], blank, taken)], axis=1)
    source = jnp.concatenate([inputs, upstream], axis=0)
    return jnp.dot(dispatch, source, preferred_element_type=jnp.float32).astype(jnp.bfloat16)


def combine(slots, wts, returned, row_slot, first):
    spread = jnp.where(slots[None, :, :] == row_slot[:, None, None], wts[None, :, :], 0.0).sum(axis=2).T
    zero = jnp.zeros_like(spread)
    weights = jnp.concatenate([jnp.where(first[None, :], spread, zero), jnp.where(first[None, :], zero, spread)], axis=0)
    parts = jnp.concatenate(split_weights(weights), axis=0)
    summed = jnp.dot(parts, returned, preferred_element_type=jnp.float32)
    return summed.reshape(2, weights.shape[0], returned.shape[1]).sum(axis=0)


def combine_half(slots, wts, returned, row_slot, side):
    spread = jnp.where(slots[None, :, :] == row_slot[:, None, None], wts[None, :, :], 0.0).sum(axis=2).T
    weights = jnp.where(side[None, :], spread, jnp.zeros_like(spread))
    parts = jnp.concatenate(split_weights(weights), axis=0)
    summed = jnp.dot(parts, returned, preferred_element_type=jnp.float32)
    return summed.reshape(2, weights.shape[0], returned.shape[1]).sum(axis=0)


def unpack(received, main, tail):
    group_size, _, width = received.shape
    inputs = [received[:, :main].reshape(group_size * main, width)]
    upstream = [received[:, main:2 * main].reshape(group_size * main, width)]
    if tail:
        ends = received[:, 2 * main:].reshape(group_size, 2, tail, width)
        inputs.append(ends[:, 0].reshape(group_size * tail, width))
        upstream.append(ends[:, 1].reshape(group_size * tail, width))
    return inputs, upstream


def repack(result, grads, group_size, main, tail):
    width = result.shape[1]
    edge = group_size * main
    pieces = [result[:edge].reshape(group_size, main, width), grads[:edge].reshape(group_size, main, width)]
    if tail:
        pieces += [result[edge:].reshape(group_size, tail, width), grads[edge:].reshape(group_size, tail, width)]
    return jnp.concatenate(pieces, axis=1)


def per_device(tokens, grad_out, expert_ids, combine_w, w_gate, w_up, w_down):
    token_count, width = tokens.shape
    top_count = expert_ids.shape[1]
    halves = lax.axis_size("half")
    subs = lax.axis_size("sub")
    group_size = lax.axis_size("node") * subs
    experts = group_size * halves
    capacity = max(2, (5 * token_count * top_count + 4 * experts - 1) // (4 * experts))
    slots_per = (capacity + 3) // 4 * 4
    main = slots_per // 8 * 8
    tail = slots_per - main
    row_slot, first = chunk_rows(group_size, slots_per)
    swap = [(i, (i + 1) % halves) for i in range(halves)]
    here = lax.axis_index("half")
    far_stacked = lax.ppermute(jnp.concatenate([tokens, grad_out], axis=0), "half", swap)
    far_ids = lax.ppermute(expert_ids, "half", swap)
    far_w = lax.ppermute(combine_w, "half", swap)

    def near_slots(ids):
        near = (ids % (halves * subs)) // subs == here
        group = (ids // (halves * subs)) * subs + ids % subs
        return route(ids, near, group, group_size, slots_per)

    both_w = jnp.concatenate([w_gate[0], w_up[0]], axis=1)
    own_slots = near_slots(expert_ids)
    far_slots = near_slots(far_ids)
    own_sent = inward(pack(own_slots, tokens, grad_out, row_slot, first).reshape(group_size, 2 * slots_per, width))
    far_stacked, far_w, own_sent = lax.optimization_barrier((far_stacked, far_w, own_sent))
    far_sent = pack(far_slots, far_stacked[:token_count], far_stacked[token_count:], row_slot, first)
    far_sent = inward(far_sent.reshape(group_size, 2 * slots_per, width))
    own_in, own_up = unpack(own_sent, main, tail)
    own_res, own_grads = expert_rows(jnp.concatenate(own_in, axis=0), jnp.concatenate(own_up, axis=0),
                                     both_w, w_down[0])
    own_packed = repack(own_res, own_grads, group_size, main, tail)
    far_in, far_up = unpack(far_sent, main, tail)
    far_res, far_grads = expert_rows(jnp.concatenate(far_in, axis=0), jnp.concatenate(far_up, axis=0),
                                     both_w, w_down[0])
    half_rows = group_size * slots_per
    far_back = inward(repack(far_res, far_grads, group_size, main, tail))
    far_back, own_packed = lax.optimization_barrier((far_back, own_packed))
    far_rows = far_back.reshape(2 * half_rows, width)
    cut = width // 2
    near_part = jnp.concatenate([jnp.concatenate([
        lax.ppermute(combine_half(far_slots, far_w, far_rows[:, cols], row_slot, side).astype(jnp.bfloat16), "half", swap)
        for cols in (slice(0, cut), slice(cut, width))], axis=1) for side in (first, ~first)], axis=0).astype(jnp.float32)
    own_back = inward(own_packed)
    own_sum = combine(own_slots, combine_w, own_back.reshape(2 * half_rows, width), row_slot, first) + near_part
    return (own_sum[:token_count].astype(jnp.bfloat16), own_sum[token_count:].astype(jnp.bfloat16))


def solution(mesh):
    nodes = mesh.shape["node"]
    locals_ = mesh.shape["local"]
    grid = jax.sharding.Mesh(mesh.devices.reshape(nodes, 2, locals_ // 2), ("node", "half", "sub"))
    rows = P(("node", "half", "sub"), None)
    stack = P(("node", "half", "sub"), None, None)
    return jax.shard_map(
        per_device,
        mesh=grid,
        in_specs=(rows, rows, rows, rows, stack, stack, stack),
        out_specs=(rows, rows),
        check_vma=False,
    )
```
